128 devices in a mesh: gx: 16 (over x_lo, y, core), gy: 8 (over z, x_hi).
Axes of the slice: x: 4 (x_hi: 2, x_lo: 2; x = x_hi * 2 + x_lo), y: 4, z: 4, core: 2. Of those that a mesh axis runs over, the one named last changes fastest.
Arguments:
- hidden: bfloat16 [16384, 1600], P('gx'), may hold values from -6 to 6
- lengths: int32 [8], replicated, may hold values from 1 to 2048, 8192 in all
- query_weight: bfloat16 [1600, 1024], P('gx', 'gy')
- key_weight: bfloat16 [1600, 1024], P('gx', 'gy'), may hold values from -0.15625 to 0.15625
- value_weight: bfloat16 [1600, 1024], P('gx', 'gy'), may hold values from -0.15625 to 0.15625
- out_weight: bfloat16 [1024, 1600], P('gy', 'gx'), may hold values from -0.1875 to 0.1875
- expand_weight: bfloat16 [1600, 6400], P('gx', 'gy'), may hold values from -0.15625 to 0.15625
- contract_weight: bfloat16 [6400, 1600], P('gy', 'gx'), may hold values from -0.078125 to 0.078125
- kv_cache: bfloat16 [16, 2, 6144, 1024], P(None, None, 'gx', 'gy'), may hold values from -6 to 6
- prompt_group: int32 [8], replicated, may hold values from 0 to 7, as said below
- page_table: int32 [8, 6], replicated, may hold values from 0 to 11, as said below
Outputs:
- output: bfloat16 [16384, 1600], P('gx', 'gy')
- decode_cache: bfloat16 [16, 8, 2, 1536, 1024], P('gx', 'gy')
The draws below stay inside these ranges and needn't reach their ends.
Inputs may be any that keep to these rules, and one draw needn't show every extreme that they name: `prompt_group`: no request group holds more than 2 prompts, and some group holds exactly 2. `page_table`: the pool slots named for the pages of the prompts of one request group are all different. `lengths`: the longest span has exactly 2048 tokens.
All inputs are finite; a program needn't handle non-finite values.
Results may differ from the reference program's by a relative error of at most 0.014.
The reference program's roundings to bfloat16 on the way count: a program that leaves them out, or rounds other values in their place, can miss the bound.
Values may be sent and summed in bfloat16 or wider, within the bound.
No kernel may reach another device: no remote copies, remote signals or barrier semaphores. Data moves between devices by JAX's collectives and lax.ppermute only.
A program may use at most 128 MiB of HBM per device.

```python
import math
import jax
import jax.numpy as jnp
import numpy as np
from jax import lax

D = 1600
HEADS = 16
HD = 64
FF = 6400
PRIOR = 768
PAGE = 128
GROUP_MOST = 2
SPAN = 2048
PROMPTS = 8
TOKENS = 16384
PTOK = 6144
LAYERS = 16
GROUPS = 8
POOL = 12


def draw_query_weight(key, part):
    base = jax.random.normal(key, (D, HEADS * HD), jnp.float32) * D ** (-0.5)
    return base.astype(jnp.bfloat16)


def place_slot(slot_perm, position, wanted, needed):
    found = jnp.argmax(slot_perm == wanted).astype(jnp.int32)
    moved = slot_perm.at[found].set(slot_perm[position]).at[position].set(wanted)
    return jnp.where(needed, moved, slot_perm)


def build_tables(key):
    key = jax.random.fold_in(key, 11)
    key_slots = jax.random.fold_in(key, 1)
    key_order = jax.random.fold_in(key, 2)
    key_pools = jax.random.fold_in(key, 3)
    slot_count = GROUP_MOST * GROUPS
    slot_perm = jax.random.permutation(key_slots, slot_count).astype(jnp.int32)
    first_slot = slot_perm[0]
    partner_slot = first_slot // GROUP_MOST * GROUP_MOST + (first_slot % GROUP_MOST + 1) % GROUP_MOST
    partner_place = jnp.argmax(slot_perm == partner_slot).astype(jnp.int32)
    second_slot = slot_perm[1]
    slot_perm = slot_perm.at[partner_place].set(second_slot).at[1].set(partner_slot)
    full_group = first_slot // GROUP_MOST
    slot_perm = place_slot(slot_perm, 2, jnp.int32(0), full_group != 0)
    slot_perm = place_slot(slot_perm, 3, jnp.int32((GROUPS - 1) * GROUP_MOST), full_group != GROUPS - 1)
    prompt_order = jax.random.permutation(key_order, PROMPTS).astype(jnp.int32)
    slot_of = jnp.zeros((PROMPTS,), jnp.int32).at[prompt_order].set(slot_perm[:PROMPTS])
    group_of = slot_of // GROUP_MOST
    rank_in = slot_of % GROUP_MOST
    pool_keys = jax.random.split(key_pools, GROUPS)
    pool_perms = jax.vmap(lambda pool_key: jax.random.permutation(pool_key, POOL))(pool_keys).astype(jnp.int32)
    pages_each = PRIOR // PAGE
    within = rank_in[:, None] * pages_each + jnp.arange(pages_each, dtype=jnp.int32)[None, :]
    page_slots = pool_perms[group_of[:, None], within]
    return (group_of.astype(jnp.int32), page_slots.astype(jnp.int32))


def draw_prompt_group(key, part):
    return build_tables(key)[0]


def draw_page_table(key, part):
    return build_tables(key)[1]


def block_levels(stream_key, shape, cuts, least, largest):
    level, own = 1.0, jax.random.fold_in(stream_key, 6)
    for dim, parts in cuts:
        draws = jnp.exp(jax.random.uniform(jax.random.fold_in(own, dim), (parts,), jnp.float32, least / len(cuts), largest / len(cuts)))
        level = level * jnp.repeat(draws, shape[dim] // parts).reshape([-1 if axis == dim else 1 for axis in range(len(shape))])
    return level


def split_up(amount, total, most, skew):
    weights = [(1 << 20) // math.isqrt(rank ** skew) + 1 for rank in range(2, amount + 1)]
    rest, counts = total - most - (amount - 1), [1] * (amount - 1)
    while rest > 0:
        candidates = [i for i in range(amount - 1) if counts[i] < most]
        whole, remaining = sum([weights[i] for i in candidates]), rest
        for i in candidates:
            addition = min(most - counts[i], max(1, remaining * weights[i] // whole), rest)
            counts[i] = counts[i] + addition
            rest = rest - addition
    return np.array([most] + counts)


def uneven(key, number_of, total, most, lean):
    if number_of == 2:
        one = jax.random.randint(key, (), max(1, total - most), min(most, total - 1) + 1)
        return jnp.stack([one, total - one])
    sizes = jnp.asarray(split_up(number_of, total, most, lean), jnp.int32)
    couples = (number_of - 1) // 2
    giver, receiver = sizes[1:1 + 2 * couples:2], sizes[2:2 + 2 * couples:2]
    room = jnp.minimum(giver - 1, most - receiver)
    shifted = jax.random.randint(jax.random.fold_in(key, 1), (couples,), 0, 1 << 20) % (room + 1)
    sizes = sizes.at[1:1 + 2 * couples:2].set(giver - shifted).at[2:2 + 2 * couples:2].set(receiver + shifted)
    return sizes[jax.random.permutation(jax.random.fold_in(key, 2), number_of)]


def scatter_about(key, shape, spread, limit, cuts=(), kind=jnp.bfloat16):
    loudness = block_levels(key, shape, cuts, -0.22, 0.18) if cuts else 1.0
    entries = jax.random.normal(key, shape, jnp.float32) * spread * loudness
    return jnp.minimum(jnp.maximum(entries, -limit), limit).astype(kind)


def setup_inputs(seed: int = 0) -> dict:
    seeds = jax.random.split(jax.random.key(seed), 12)
    return {
        "hidden": scatter_about(seeds[0], (TOKENS, D), 1.0, 6.0, ((0, 16),)),
        "lengths": uneven(seeds[1], PROMPTS, TOKENS // 2, SPAN, 2).astype(jnp.int32),
        "query_weight": draw_query_weight(jax.random.fold_in(seeds[11], 71), 0),
        "key_weight": scatter_about(seeds[3], (D, HEADS * HD), D ** -0.5, 0.15625, ((0, 16), (1, 8))),
        "value_weight": scatter_about(seeds[4], (D, HEADS * HD), D ** -0.5, 0.15625, ((0, 16), (1, 8))),
        "out_weight": scatter_about(seeds[5], (HEADS * HD, D), (HEADS * HD) ** -0.5, 0.1875, ((0, 8), (1, 16))),
        "expand_weight": scatter_about(seeds[6], (D, FF), D ** -0.5, 0.15625, ((0, 16), (1, 8))),
        "contract_weight": scatter_about(seeds[7], (FF, D), FF ** -0.5, 0.078125, ((0, 8), (1, 16))),
        "kv_cache": scatter_about(seeds[8], (LAYERS, 2, PTOK, HEADS * HD), 1.0, 6.0, ((2, 16), (3, 8))),
        "prompt_group": draw_prompt_group(jax.random.fold_in(seeds[11], 71), 0),
        "page_table": draw_page_table(jax.random.fold_in(seeds[11], 71), 0),
    }


EPSILON = 1e-05

def normalized(row_block):
    row_sum = lax.optimization_barrier(jnp.sum(row_block, axis=1, keepdims=True))
    row_squares = lax.optimization_barrier(jnp.sum(row_block * row_block, axis=1, keepdims=True))
    average = row_sum / D
    variance = row_squares / D - average * average
    return (row_block - average) * lax.rsqrt(variance + EPSILON)

def attend_head(query_head, key_head, value_head, allowed):
    scores = jnp.einsum('sd,kd->sk', query_head, key_head.astype(jnp.float32), precision=lax.Precision.HIGHEST) * HD ** (-0.5)
    scores = jnp.where(allowed, scores, -jnp.inf)
    highest = lax.optimization_barrier(jnp.max(scores, axis=1, keepdims=True))
    weights = jnp.exp(scores - highest)
    weight_sum = lax.optimization_barrier(jnp.sum(weights, axis=1, keepdims=True))
    mixed_rows = jnp.dot(weights.astype(jnp.bfloat16), value_head, preferred_element_type=jnp.float32)
    return mixed_rows / weight_sum

def one_prompt(prompt, hidden, lengths, query_weight, key_weight, value_weight, out_weight, expand_weight, contract_weight, kv_cache):
    row_start = (prompt * SPAN).astype(jnp.int32)
    span_rows = lax.dynamic_slice_in_dim(hidden, row_start, SPAN, 0).astype(jnp.float32)
    normed = normalized(span_rows).astype(jnp.bfloat16)
    queries = jnp.dot(normed, query_weight, preferred_element_type=jnp.float32)
    new_keys = jnp.dot(normed, key_weight, preferred_element_type=jnp.float32).astype(jnp.bfloat16)
    new_values = jnp.dot(normed, value_weight, preferred_element_type=jnp.float32).astype(jnp.bfloat16)
    prior_start = (prompt * PRIOR).astype(jnp.int32)
    prior_keys = lax.dynamic_slice_in_dim(kv_cache[0, 0], prior_start, PRIOR, 0)
    prior_values = lax.dynamic_slice_in_dim(kv_cache[0, 1], prior_start, PRIOR, 0)
    all_keys = jnp.concatenate([prior_keys, new_keys], axis=0)
    all_values = jnp.concatenate([prior_values, new_values], axis=0)
    positions = jnp.arange(SPAN, dtype=jnp.int32)
    allowed = jnp.concatenate([jnp.ones((SPAN, PRIOR), dtype=bool), positions[None, :] <= positions[:, None]], axis=1)
    pieces = []
    for head_index in range(HEADS):
        columns = slice(head_index * HD, (head_index + 1) * HD)
        pieces.append(attend_head(queries[:, columns], all_keys[:, columns], all_values[:, columns], allowed))
    attended = jnp.concatenate(pieces, axis=1).astype(jnp.bfloat16)
    residual = span_rows + jnp.dot(attended, out_weight, preferred_element_type=jnp.float32)
    normed_two = normalized(residual).astype(jnp.bfloat16)
    expanded = jax.nn.gelu(jnp.dot(normed_two, expand_weight, preferred_element_type=jnp.float32), approximate=True).astype(jnp.bfloat16)
    result = residual + jnp.dot(expanded, contract_weight, preferred_element_type=jnp.float32)
    is_valid = positions < lengths[prompt]
    return jnp.where(is_valid[:, None], result, 0.0).astype(jnp.bfloat16)

def hand_over(kv_cache, prompt_group, page_table):
    pages_each = PRIOR // PAGE
    total_pages = PROMPTS * pages_each
    page_ids = jnp.arange(total_pages, dtype=jnp.int32)
    destination = prompt_group[page_ids // pages_each] * POOL + page_table.reshape(-1)
    source = jnp.full((GROUPS * POOL,), -1, jnp.int32).at[destination].set(page_ids)
    page_blocks = kv_cache.reshape(LAYERS, 2, total_pages, PAGE, HEADS * HD)
    picked = jnp.take(page_blocks, jnp.maximum(source, 0), axis=2)
    picked = jnp.where((source >= 0)[None, None, :, None, None], picked, jnp.zeros((), picked.dtype))
    picked = picked.reshape(LAYERS, 2, GROUPS, POOL * PAGE, HEADS * HD)
    return jnp.transpose(picked, (0, 2, 1, 3, 4))

def reference(hidden, lengths, query_weight, key_weight, value_weight, out_weight, expand_weight, contract_weight, kv_cache, prompt_group, page_table):

    def step_prompt(prompt):
        return one_prompt(prompt, hidden, lengths, query_weight, key_weight, value_weight, out_weight, expand_weight, contract_weight, kv_cache)
    outputs = lax.map(step_prompt, jnp.arange(PROMPTS, dtype=jnp.int32))
    output = outputs.reshape(TOKENS, D)
    return (output, hand_over(kv_cache, prompt_group, page_table))
```

```python
import jax
import jax.numpy as jnp
from jax import lax
from jax.sharding import PartitionSpec as P

D = 1600
HD = 64
PRIOR = 768
PAGE = 128
POOL = 12


EPSILON = 1e-05

GX_CORE = (1, 2)
GX_Y = (2, 4)
GX_XLO = (8, 2)
GY_XHI = (1, 2)
GY_Z = (2, 4)


def shift_pairs(count, stride, size, step):
    pairs = []
    for i in range(count):
        c = (i // stride) % size
        j = i + (((c + step) % size) - c) * stride
        if j != i:
            pairs.append((i, j))
    return pairs


def sub_gather(block, axis, sub):
    stride, size = sub
    count = lax.axis_size(axis)
    c = (lax.axis_index(axis) // stride) % size
    if size == 2:
        other = lax.ppermute(block, axis, shift_pairs(count, stride, size, 1))
        got = jnp.stack([block, other])
    else:
        from_left = lax.ppermute(block, axis, shift_pairs(count, stride, size, 1))
        from_right = lax.ppermute(block, axis, shift_pairs(count, stride, size, -1))
        from_two = lax.ppermute(from_left, axis, shift_pairs(count, stride, size, 1))
        got = jnp.stack([block, from_left, from_two, from_right])
    order = (c - jnp.arange(size, dtype=jnp.int32)) % size
    return jnp.take(got, order, axis=0)


def gather_gx(block):
    g = sub_gather(block, "gx", GX_CORE)
    g = sub_gather(g, "gx", GX_XLO)
    g = sub_gather(g, "gx", GX_Y)
    g = jnp.swapaxes(g, 0, 1)
    return g.reshape((-1,) + block.shape)


def gather_gy(block):
    g = sub_gather(block, "gy", GY_XHI)
    g = sub_gather(g, "gy", GY_Z)
    return g.reshape((-1,) + block.shape)


def reduce_scatter_gy(blocks):
    count = lax.axis_size("gy")
    idx = lax.axis_index("gy")
    z = idx // 2
    h = idx % 2
    zsize = GY_Z[1]
    by_z = blocks.reshape((zsize, 2) + blocks.shape[1:])
    total = lax.dynamic_index_in_dim(by_z, z, 0, keepdims=False)
    for step in range(1, zsize):
        outgoing = lax.dynamic_index_in_dim(by_z, (z + step) % zsize, 0, keepdims=False)
        arrived = lax.ppermute(
            outgoing.astype(jnp.bfloat16), "gy", shift_pairs(count, GY_Z[0], zsize, step)
        )
        total = total + arrived.astype(jnp.float32)
    keep = lax.dynamic_index_in_dim(total, h, 0, keepdims=False)
    give = lax.dynamic_index_in_dim(total, 1 - h, 0, keepdims=False)
    arrived = lax.ppermute(give.astype(jnp.bfloat16), "gy", shift_pairs(count, 1, 2, 1))
    return keep + arrived.astype(jnp.float32)


def finish_norm(row_block, row_sum, row_squares):
    average = row_sum / D
    variance = row_squares / D - average * average
    return (row_block - average) * lax.rsqrt(variance + EPSILON)


def normalized(row_block):
    return finish_norm(
        row_block,
        jnp.sum(row_block, axis=1, keepdims=True),
        jnp.sum(row_block * row_block, axis=1, keepdims=True),
    )


def ordered(own_part, other_part, is_first):
    lower_part = jnp.where(is_first, own_part, other_part)
    upper_part = jnp.where(is_first, other_part, own_part)
    return jnp.concatenate([lower_part, upper_part], axis=0)


def hand_over(kv_cache, prompt_group, page_table):
    moved_pages = lax.all_to_all(kv_cache, "gx", split_axis=0, concat_axis=2, tiled=True)
    columns = moved_pages.shape[3]
    pages_each = PRIOR // PAGE
    total_pages = moved_pages.shape[2] // PAGE
    groups = lax.axis_size("gy")
    page_ids = jnp.arange(total_pages, dtype=jnp.int32)
    destination = prompt_group[page_ids // pages_each] * POOL + page_table.reshape(-1)
    source = jnp.full((groups * POOL,), -1, jnp.int32).at[destination].set(page_ids)
    page_blocks = moved_pages.reshape(2, total_pages, PAGE, columns)
    picked = jnp.take(page_blocks, jnp.maximum(source, 0), axis=1)
    picked = jnp.where((source >= 0)[None, :, None, None], picked, jnp.zeros((), picked.dtype))
    picked = picked.reshape(2, groups, POOL, PAGE, columns)
    arrived = lax.all_to_all(picked, "gy", split_axis=1, concat_axis=4, tiled=True)
    return arrived.reshape(1, 1, 2, POOL * PAGE, columns * groups)


def on_device(
    hidden,
    lengths,
    query_weight,
    key_weight,
    value_weight,
    out_weight,
    expand_weight,
    contract_weight,
    kv_cache,
    prompt_group,
    page_table,
):
    slot_count = hidden.shape[0]
    device_row = lax.axis_index("gx")
    is_first = device_row % 2 == 0
    prompt = device_row // 2
    offset = device_row % 2 * slot_count
    local_cols = query_weight.shape[1]

    qkv_block = jnp.concatenate([query_weight, key_weight, value_weight], axis=1)
    qkv_full = gather_gx(qkv_block).reshape(D, 3 * local_cols)
    query_full = qkv_full[:, :local_cols]
    key_full = qkv_full[:, local_cols : 2 * local_cols]
    value_full = qkv_full[:, 2 * local_cols :]

    out_cols = jnp.moveaxis(gather_gx(out_weight), 0, 1).reshape(out_weight.shape[0], D)
    out_full = gather_gy(out_cols).reshape(-1, D)

    ffn_block = jnp.concatenate([expand_weight, contract_weight.T], axis=1)
    ffn_full = gather_gx(ffn_block).reshape(D, -1)
    ff_cols = expand_weight.shape[1]
    expand_full = ffn_full[:, :ff_cols]
    contract_full_t = ffn_full[:, ff_cols:]

    rows_full = hidden.astype(jnp.float32)
    normed = normalized(rows_full).astype(jnp.bfloat16)
    queries = jnp.dot(normed, query_full, preferred_element_type=jnp.float32)
    new_keys = jnp.dot(normed, key_full, preferred_element_type=jnp.float32).astype(jnp.bfloat16)
    new_values = jnp.dot(normed, value_full, preferred_element_type=jnp.float32).astype(
        jnp.bfloat16
    )
    prior_keys = kv_cache[0, 0]
    prior_values = kv_cache[0, 1]
    partner = lax.ppermute(
        (new_keys, new_values, prior_keys, prior_values),
        "gx",
        shift_pairs(lax.axis_size("gx"), 1, 2, 1),
    )
    all_keys = jnp.concatenate(
        [ordered(prior_keys, partner[2], is_first), ordered(new_keys, partner[0], is_first)], axis=0
    )
    all_values = jnp.concatenate(
        [ordered(prior_values, partner[3], is_first), ordered(new_values, partner[1], is_first)],
        axis=0,
    )
    prior_count = 2 * prior_keys.shape[0]
    query_pos = offset + jnp.arange(slot_count, dtype=jnp.int32)
    key_pos = jnp.arange(2 * slot_count, dtype=jnp.int32)
    allowed = jnp.concatenate(
        [jnp.ones((slot_count, prior_count), dtype=bool), key_pos[None, :] <= query_pos[:, None]],
        axis=1,
    )
    local_heads = queries.shape[1] // HD

    def split_heads(matrix):
        return matrix.reshape(matrix.shape[0], local_heads, HD).transpose(1, 0, 2)

    def one_head(operands):
        query_head, key_head, value_head = operands
        scores = jnp.einsum(
            "sd,kd->sk", query_head, key_head.astype(jnp.float32), precision=lax.Precision.HIGHEST
        ) * HD ** (-0.5)
        scores = jnp.where(allowed, scores, -jnp.inf)
        highest = jnp.max(scores, axis=1, keepdims=True)
        weights = jnp.exp(scores - highest)
        weight_sum = jnp.sum(weights, axis=1, keepdims=True)
        mixed_rows = jnp.dot(
            weights.astype(jnp.bfloat16), value_head, preferred_element_type=jnp.float32
        )
        return mixed_rows / weight_sum

    attended = lax.map(
        one_head, (split_heads(queries), split_heads(all_keys), split_heads(all_values))
    )
    attended = (
        attended.transpose(1, 0, 2).reshape(slot_count, local_heads * HD).astype(jnp.bfloat16)
    )
    attended_all = gather_gy(attended)
    attended_all = jnp.moveaxis(attended_all, 0, 1).reshape(slot_count, -1)
    residual = rows_full + jnp.dot(attended_all, out_full, preferred_element_type=jnp.float32)
    normed_two = normalized(residual).astype(jnp.bfloat16)
    expanded = jax.nn.gelu(
        jnp.dot(normed_two, expand_full, preferred_element_type=jnp.float32), approximate=True
    ).astype(jnp.bfloat16)
    contracted = lax.dot_general(
        expanded, contract_full_t, (((1,), (1,)), ((), ())), preferred_element_type=jnp.float32
    )
    groups = lax.axis_size("gy")
    own_width = D // groups
    blocks = contracted.reshape(slot_count, groups, own_width).transpose(1, 0, 2)
    summed = reduce_scatter_gy(blocks)
    column_start = lax.axis_index("gy") * own_width
    residual_own = lax.dynamic_slice_in_dim(residual, column_start, own_width, 1)
    is_valid = query_pos < lengths[prompt]
    output = jnp.where(is_valid[:, None], residual_own + summed, 0.0).astype(jnp.bfloat16)
    return (output, hand_over(kv_cache, prompt_group, page_table))


def solution(mesh):
    placed = (
        P("gx", None),
        P(),
        P("gx", "gy"),
        P("gx", "gy"),
        P("gx", "gy"),
        P("gy", "gx"),
        P("gx", "gy"),
        P("gy", "gx"),
        P(None, None, "gx", "gy"),
        P(),
        P(),
    )
    return jax.shard_map(
        on_device,
        mesh=mesh,
        in_specs=placed,
        out_specs=(P("gx", "gy"), P("gx", "gy", None, None, None)),
        check_vma=False,
    )
```

```python
import jax
import jax.numpy as jnp
from jax import lax
from jax.sharding import PartitionSpec as P

D = 1600
HD = 64
PRIOR = 768
PAGE = 128
POOL = 12


EPSILON = 1e-05

GX_CORE = (1, 2)
GX_Y = (2, 4)
GX_XLO = (8, 2)
GY_XHI = (1, 2)
GY_Z = (2, 4)


def shift_pairs(count, stride, size, step):
    pairs = []
    for i in range(count):
        c = (i // stride) % size
        j = i + (((c + step) % size) - c) * stride
        if j != i:
            pairs.append((i, j))
    return pairs


def sub_gather(block, axis, sub):
    stride, size = sub
    count = lax.axis_size(axis)
    c = (lax.axis_index(axis) // stride) % size
    if size == 2:
        other = lax.ppermute(block, axis, shift_pairs(count, stride, size, 1))
        got = jnp.stack([block, other])
    else:
        from_left = lax.ppermute(block, axis, shift_pairs(count, stride, size, 1))
        from_right = lax.ppermute(block, axis, shift_pairs(count, stride, size, -1))
        from_two = lax.ppermute(from_left, axis, shift_pairs(count, stride, size, 1))
        got = jnp.stack([block, from_left, from_two, from_right])
    order = (c - jnp.arange(size, dtype=jnp.int32)) % size
    return jnp.take(got, order, axis=0)


def gather_gx(block):
    g = sub_gather(block, "gx", GX_CORE)
    g = sub_gather(g, "gx", GX_XLO)
    g = sub_gather(g, "gx", GX_Y)
    g = jnp.swapaxes(g, 0, 1)
    return g.reshape((-1,) + block.shape)


def gather_gy(block):
    g = sub_gather(block, "gy", GY_XHI)
    g = sub_gather(g, "gy", GY_Z)
    return g.reshape((-1,) + block.shape)


def reduce_scatter_gy(blocks):
    count = lax.axis_size("gy")
    idx = lax.axis_index("gy")
    z = idx // 2
    h = idx % 2
    zsize = GY_Z[1]
    by_z = blocks.reshape((zsize, 2) + blocks.shape[1:])
    total = lax.dynamic_index_in_dim(by_z, z, 0, keepdims=False)
    for step in range(1, zsize):
        outgoing = lax.dynamic_index_in_dim(by_z, (z + step) % zsize, 0, keepdims=False)
        arrived = lax.ppermute(
            outgoing.astype(jnp.bfloat16), "gy", shift_pairs(count, GY_Z[0], zsize, step)
        )
        total = total + arrived.astype(jnp.float32)
    keep = lax.dynamic_index_in_dim(total, h, 0, keepdims=False)
    give = lax.dynamic_index_in_dim(total, 1 - h, 0, keepdims=False)
    arrived = lax.ppermute(give.astype(jnp.bfloat16), "gy", shift_pairs(count, 1, 2, 1))
    return keep + arrived.astype(jnp.float32)


def direct_gather(block, axis):
    count = lax.axis_size(axis)
    idx = lax.axis_index(axis)
    got = [block]
    for step in range(1, count):
        got.append(lax.ppermute(block, axis, [(i, (i + step) % count) for i in range(count)]))
    order = (idx - jnp.arange(count, dtype=jnp.int32)) % count
    return jnp.take(jnp.stack(got), order, axis=0)


def direct_reduce_scatter(blocks, axis):
    count = lax.axis_size(axis)
    idx = lax.axis_index(axis)
    total = lax.dynamic_index_in_dim(blocks, idx, 0, keepdims=False)
    for step in range(1, count):
        outgoing = lax.dynamic_index_in_dim(blocks, (idx + step) % count, 0, keepdims=False)
        arrived = lax.ppermute(
            outgoing.astype(jnp.bfloat16), axis, [(i, (i + step) % count) for i in range(count)]
        )
        total = total + arrived.astype(jnp.float32)
    return total


def finish_norm(row_block, row_sum, row_squares):
    average = row_sum / D
    variance = row_squares / D - average * average
    return (row_block - average) * lax.rsqrt(variance + EPSILON)


def normalized(row_block):
    return finish_norm(
        row_block,
        jnp.sum(row_block, axis=1, keepdims=True),
        jnp.sum(row_block * row_block, axis=1, keepdims=True),
    )


def ordered(own_part, other_part, is_first):
    lower_part = jnp.where(is_first, own_part, other_part)
    upper_part = jnp.where(is_first, other_part, own_part)
    return jnp.concatenate([lower_part, upper_part], axis=0)


def hand_over(kv_cache, prompt_group, page_table):
    moved_pages = lax.all_to_all(kv_cache, "gx", split_axis=0, concat_axis=2, tiled=True)
    columns = moved_pages.shape[3]
    pages_each = PRIOR // PAGE
    total_pages = moved_pages.shape[2] // PAGE
    groups = lax.axis_size("gy")
    page_ids = jnp.arange(total_pages, dtype=jnp.int32)
    destination = prompt_group[page_ids // pages_each] * POOL + page_table.reshape(-1)
    source = jnp.full((groups * POOL,), -1, jnp.int32).at[destination].set(page_ids)
    page_blocks = moved_pages.reshape(2, total_pages, PAGE, columns)
    picked = jnp.take(page_blocks, jnp.maximum(source, 0), axis=1)
    picked = jnp.where((source >= 0)[None, :, None, None], picked, jnp.zeros((), picked.dtype))
    picked = picked.reshape(2, groups, POOL * PAGE, columns)
    group = lax.axis_index("gy")
    got = [lax.dynamic_index_in_dim(picked, group, 1, keepdims=False)]
    for step in range(1, groups):
        outgoing = lax.dynamic_index_in_dim(picked, (group + step) % groups, 1, keepdims=False)
        got.append(lax.ppermute(outgoing, "gy", [(i, (i + step) % groups) for i in range(groups)]))
    order = (group - jnp.arange(groups, dtype=jnp.int32)) % groups
    arrived = jnp.take(jnp.stack(got, axis=2), order, axis=2)
    return arrived.reshape(1, 1, 2, POOL * PAGE, columns * groups)


def on_device(
    hidden,
    lengths,
    query_weight,
    key_weight,
    value_weight,
    out_weight,
    expand_weight,
    contract_weight,
    kv_cache,
    prompt_group,
    page_table,
):
    slot_count = hidden.shape[0]
    device_row = lax.axis_index("gx")
    is_first = device_row % 2 == 0
    prompt = device_row // 2
    offset = device_row % 2 * slot_count
    local_cols = query_weight.shape[1]

    qkv_block = jnp.concatenate([query_weight, key_weight, value_weight], axis=1)
    qkv_full = direct_gather(qkv_block, "gx").reshape(D, 3 * local_cols)
    query_full = qkv_full[:, :local_cols]
    key_full = qkv_full[:, local_cols : 2 * local_cols]
    value_full = qkv_full[:, 2 * local_cols :]

    out_cols = jnp.moveaxis(direct_gather(out_weight, "gx"), 0, 1).reshape(out_weight.shape[0], D)
    out_full = direct_gather(out_cols, "gy").reshape(-1, D)

    ffn_block = jnp.concatenate([expand_weight, contract_weight.T], axis=1)
    ffn_full = direct_gather(ffn_block, "gx").reshape(D, -1)
    ff_cols = expand_weight.shape[1]
    expand_full = ffn_full[:, :ff_cols]
    contract_full_t = ffn_full[:, ff_cols:]

    rows_full = hidden.astype(jnp.float32)
    normed = normalized(rows_full).astype(jnp.bfloat16)
    queries = jnp.dot(normed, query_full, preferred_element_type=jnp.float32)
    new_keys = jnp.dot(normed, key_full, preferred_element_type=jnp.float32).astype(jnp.bfloat16)
    new_values = jnp.dot(normed, value_full, preferred_element_type=jnp.float32).astype(
        jnp.bfloat16
    )
    prior_keys = kv_cache[0, 0]
    prior_values = kv_cache[0, 1]
    partner = lax.ppermute(
        (new_keys, new_values, prior_keys, prior_values),
        "gx",
        shift_pairs(lax.axis_size("gx"), 1, 2, 1),
    )
    all_keys = jnp.concatenate(
        [ordered(prior_keys, partner[2], is_first), ordered(new_keys, partner[0], is_first)], axis=0
    )
    all_values = jnp.concatenate(
        [ordered(prior_values, partner[3], is_first), ordered(new_values, partner[1], is_first)],
        axis=0,
    )
    prior_count = 2 * prior_keys.shape[0]
    query_pos = offset + jnp.arange(slot_count, dtype=jnp.int32)
    key_pos = jnp.arange(2 * slot_count, dtype=jnp.int32)
    allowed = jnp.concatenate(
        [jnp.ones((slot_count, prior_count), dtype=bool), key_pos[None, :] <= query_pos[:, None]],
        axis=1,
    )
    local_heads = queries.shape[1] // HD

    def split_heads(matrix):
        return matrix.reshape(matrix.shape[0], local_heads, HD).transpose(1, 0, 2)

    def one_head(operands):
        query_head, key_head, value_head = operands
        scores = jnp.einsum(
            "sd,kd->sk", query_head, key_head.astype(jnp.float32), precision=lax.Precision.HIGHEST
        ) * HD ** (-0.5)
        scores = jnp.where(allowed, scores, -jnp.inf)
        highest = jnp.max(scores, axis=1, keepdims=True)
        weights = jnp.exp(scores - highest)
        weight_sum = jnp.sum(weights, axis=1, keepdims=True)
        mixed_rows = jnp.dot(
            weights.astype(jnp.bfloat16), value_head, preferred_element_type=jnp.float32
        )
        return mixed_rows / weight_sum

    attended = lax.map(
        one_head, (split_heads(queries), split_heads(all_keys), split_heads(all_values))
    )
    attended = (
        attended.transpose(1, 0, 2).reshape(slot_count, local_heads * HD).astype(jnp.bfloat16)
    )
    attended_all = direct_gather(attended, "gy")
    attended_all = jnp.moveaxis(attended_all, 0, 1).reshape(slot_count, -1)
    residual = rows_full + jnp.dot(attended_all, out_full, preferred_element_type=jnp.float32)
    normed_two = normalized(residual).astype(jnp.bfloat16)
    expanded = jax.nn.gelu(
        jnp.dot(normed_two, expand_full, preferred_element_type=jnp.float32), approximate=True
    ).astype(jnp.bfloat16)
    contracted = lax.dot_general(
        expanded, contract_full_t, (((1,), (1,)), ((), ())), preferred_element_type=jnp.float32
    )
    groups = lax.axis_size("gy")
    own_width = D // groups
    blocks = contracted.reshape(slot_count, groups, own_width).transpose(1, 0, 2)
    summed = direct_reduce_scatter(blocks, "gy")
    column_start = lax.axis_index("gy") * own_width
    residual_own = lax.dynamic_slice_in_dim(residual, column_start, own_width, 1)
    is_valid = query_pos < lengths[prompt]
    output = jnp.where(is_valid[:, None], residual_own + summed, 0.0).astype(jnp.bfloat16)
    return (output, hand_over(kv_cache, prompt_group, page_table))


def solution(mesh):
    placed = (
        P("gx", None),
        P(),
        P("gx", "gy"),
        P("gx", "gy"),
        P("gx", "gy"),
        P("gy", "gx"),
        P("gx", "gy"),
        P("gy", "gx"),
        P(None, None, "gx", "gy"),
        P(),
        P(),
    )
    return jax.shard_map(
        on_device,
        mesh=mesh,
        in_specs=placed,
        out_specs=(P("gx", "gy"), P("gx", "gy", None, None, None)),
        check_vma=False,
    )
```

```python
import jax
import jax.numpy as jnp
from jax import lax
from jax.sharding import PartitionSpec as P

D = 1600
HD = 64
PRIOR = 768
PAGE = 128
POOL = 12


EPSILON = 1e-05

GX_CORE = (1, 2)
GX_Y = (2, 4)
GX_XLO = (8, 2)
GY_XHI = (1, 2)
GY_Z = (2, 4)


def shift_pairs(count, stride, size, step):
    pairs = []
    for i in range(count):
        c = (i // stride) % size
        j = i + (((c + step) % size) - c) * stride
        if j != i:
            pairs.append((i, j))
    return pairs


def sub_gather(block, axis, sub):
    stride, size = sub
    count = lax.axis_size(axis)
    c = (lax.axis_index(axis) // stride) % size
    if size == 2:
        other = lax.ppermute(block, axis, shift_pairs(count, stride, size, 1))
        got = jnp.stack([block, other])
    else:
        from_left = lax.ppermute(block, axis, shift_pairs(count, stride, size, 1))
        from_right = lax.ppermute(block, axis, shift_pairs(count, stride, size, -1))
        from_two = lax.ppermute(from_left, axis, shift_pairs(count, stride, size, 1))
        got = jnp.stack([block, from_left, from_two, from_right])
    order = (c - jnp.arange(size, dtype=jnp.int32)) % size
    return jnp.take(got, order, axis=0)


def gather_gx(block):
    g = sub_gather(block, "gx", GX_CORE)
    g = sub_gather(g, "gx", GX_XLO)
    g = sub_gather(g, "gx", GX_Y)
    g = jnp.swapaxes(g, 0, 1)
    return g.reshape((-1,) + block.shape)


def gather_gy(block):
    g = sub_gather(block, "gy", GY_XHI)
    g = sub_gather(g, "gy", GY_Z)
    return g.reshape((-1,) + block.shape)


def reduce_scatter_gy(blocks):
    count = lax.axis_size("gy")
    idx = lax.axis_index("gy")
    z = idx // 2
    h = idx % 2
    zsize = GY_Z[1]
    by_z = blocks.reshape((zsize, 2) + blocks.shape[1:])
    total = lax.dynamic_index_in_dim(by_z, z, 0, keepdims=False)
    for step in range(1, zsize):
        outgoing = lax.dynamic_index_in_dim(by_z, (z + step) % zsize, 0, keepdims=False)
        arrived = lax.ppermute(
            outgoing.astype(jnp.bfloat16), "gy", shift_pairs(count, GY_Z[0], zsize, step)
        )
        total = total + arrived.astype(jnp.float32)
    keep = lax.dynamic_index_in_dim(total, h, 0, keepdims=False)
    give = lax.dynamic_index_in_dim(total, 1 - h, 0, keepdims=False)
    arrived = lax.ppermute(give.astype(jnp.bfloat16), "gy", shift_pairs(count, 1, 2, 1))
    return keep + arrived.astype(jnp.float32)


def finish_norm(row_block, row_sum, row_squares):
    average = row_sum / D
    variance = row_squares / D - average * average
    return (row_block - average) * lax.rsqrt(variance + EPSILON)


def normalized(row_block):
    return finish_norm(
        row_block,
        jnp.sum(row_block, axis=1, keepdims=True),
        jnp.sum(row_block * row_block, axis=1, keepdims=True),
    )


def ordered(own_part, other_part, is_first):
    lower_part = jnp.where(is_first, own_part, other_part)
    upper_part = jnp.where(is_first, other_part, own_part)
    return jnp.concatenate([lower_part, upper_part], axis=0)


def hand_over(kv_cache, prompt_group, page_table):
    moved_pages = lax.all_to_all(kv_cache, "gx", split_axis=0, concat_axis=2, tiled=True)
    columns = moved_pages.shape[3]
    pages_each = PRIOR // PAGE
    total_pages = moved_pages.shape[2] // PAGE
    groups = lax.axis_size("gy")
    page_ids = jnp.arange(total_pages, dtype=jnp.int32)
    destination = prompt_group[page_ids // pages_each] * POOL + page_table.reshape(-1)
    source = jnp.full((groups * POOL,), -1, jnp.int32).at[destination].set(page_ids)
    page_blocks = moved_pages.reshape(2, total_pages, PAGE, columns)
    picked = jnp.take(page_blocks, jnp.maximum(source, 0), axis=1)
    picked = jnp.where((source >= 0)[None, :, None, None], picked, jnp.zeros((), picked.dtype))
    picked = picked.reshape(2, groups, POOL * PAGE, columns)
    arrived = lax.all_to_all(picked, "gy", split_axis=1, concat_axis=1, tiled=True)
    arrived = arrived.transpose(0, 2, 1, 3)
    return arrived.reshape(1, 1, 2, POOL * PAGE, columns * groups)


def on_device(
    hidden,
    lengths,
    query_weight,
    key_weight,
    value_weight,
    out_weight,
    expand_weight,
    contract_weight,
    kv_cache,
    prompt_group,
    page_table,
):
    slot_count = hidden.shape[0]
    device_row = lax.axis_index("gx")
    is_first = device_row % 2 == 0
    prompt = device_row // 2
    offset = device_row % 2 * slot_count
    local_cols = query_weight.shape[1]

    qkv_block = jnp.concatenate([query_weight, key_weight, value_weight], axis=1)
    qkv_full = gather_gx(qkv_block).reshape(D, 3 * local_cols)
    query_full = qkv_full[:, :local_cols]
    key_full = qkv_full[:, local_cols : 2 * local_cols]
    value_full = qkv_full[:, 2 * local_cols :]

    ffn_block = jnp.concatenate([expand_weight, contract_weight.T], axis=1)
    qkv_full, ffn_block, kv_cache = lax.optimization_barrier((qkv_full, ffn_block, kv_cache))

    out_cols = jnp.moveaxis(gather_gx(out_weight), 0, 1).reshape(out_weight.shape[0], D)
    out_full = gather_gy(out_cols).reshape(-1, D)

    ffn_full = gather_gx(ffn_block).reshape(D, -1)
    ff_cols = expand_weight.shape[1]
    expand_full = ffn_full[:, :ff_cols]
    contract_full_t = ffn_full[:, ff_cols:]

    rows_full = hidden.astype(jnp.float32)
    normed = normalized(rows_full).astype(jnp.bfloat16)
    queries = jnp.dot(normed, query_full, preferred_element_type=jnp.float32)
    new_keys = jnp.dot(normed, key_full, preferred_element_type=jnp.float32).astype(jnp.bfloat16)
    new_values = jnp.dot(normed, value_full, preferred_element_type=jnp.float32).astype(
        jnp.bfloat16
    )
    prior_keys = kv_cache[0, 0]
    prior_values = kv_cache[0, 1]
    partner = lax.ppermute(
        (new_keys, new_values, prior_keys, prior_values),
        "gx",
        shift_pairs(lax.axis_size("gx"), 1, 2, 1),
    )
    all_keys = jnp.concatenate(
        [ordered(prior_keys, partner[2], is_first), ordered(new_keys, partner[0], is_first)], axis=0
    )
    all_values = jnp.concatenate(
        [ordered(prior_values, partner[3], is_first), ordered(new_values, partner[1], is_first)],
        axis=0,
    )
    prior_count = 2 * prior_keys.shape[0]
    query_pos = offset + jnp.arange(slot_count, dtype=jnp.int32)
    key_pos = jnp.arange(2 * slot_count, dtype=jnp.int32)
    allowed = jnp.concatenate(
        [jnp.ones((slot_count, prior_count), dtype=bool), key_pos[None, :] <= query_pos[:, None]],
        axis=1,
    )
    local_heads = queries.shape[1] // HD

    def split_heads(matrix):
        return matrix.reshape(matrix.shape[0], local_heads, HD).transpose(1, 0, 2)

    def one_head(operands):
        query_head, key_head, value_head = operands
        scores = jnp.einsum(
            "sd,kd->sk", query_head, key_head.astype(jnp.float32), precision=lax.Precision.HIGHEST
        ) * HD ** (-0.5)
        scores = jnp.where(allowed, scores, -jnp.inf)
        highest = jnp.max(scores, axis=1, keepdims=True)
        weights = jnp.exp(scores - highest)
        weight_sum = jnp.sum(weights, axis=1, keepdims=True)
        mixed_rows = jnp.dot(
            weights.astype(jnp.bfloat16), value_head, preferred_element_type=jnp.float32
        )
        return mixed_rows / weight_sum

    attended = lax.map(
        one_head, (split_heads(queries), split_heads(all_keys), split_heads(all_values))
    )
    attended = (
        attended.transpose(1, 0, 2).reshape(slot_count, local_heads * HD).astype(jnp.bfloat16)
    )
    attended_all = gather_gy(attended)
    attended_all = jnp.moveaxis(attended_all, 0, 1).reshape(slot_count, -1)
    residual = rows_full + jnp.dot(attended_all, out_full, preferred_element_type=jnp.float32)
    normed_two = normalized(residual).astype(jnp.bfloat16)
    expanded = jax.nn.gelu(
        jnp.dot(normed_two, expand_full, preferred_element_type=jnp.float32), approximate=True
    ).astype(jnp.bfloat16)
    contracted = lax.dot_general(
        expanded, contract_full_t, (((1,), (1,)), ((), ())), preferred_element_type=jnp.float32
    )
    groups = lax.axis_size("gy")
    own_width = D // groups
    blocks = contracted.reshape(slot_count, groups, own_width).transpose(1, 0, 2)
    summed = reduce_scatter_gy(blocks)
    column_start = lax.axis_index("gy") * own_width
    residual_own = lax.dynamic_slice_in_dim(residual, column_start, own_width, 1)
    is_valid = query_pos < lengths[prompt]
    output = jnp.where(is_valid[:, None], residual_own + summed, 0.0).astype(jnp.bfloat16)
    return (output, hand_over(kv_cache, prompt_group, page_table))


def solution(mesh):
    placed = (
        P("gx", None),
        P(),
        P("gx", "gy"),
        P("gx", "gy"),
        P("gx", "gy"),
        P("gy", "gx"),
        P("gx", "gy"),
        P("gy", "gx"),
        P(None, None, "gx", "gy"),
        P(),
        P(),
    )
    return jax.shard_map(
        on_device,
        mesh=mesh,
        in_specs=placed,
        out_specs=(P("gx", "gy"), P("gx", "gy", None, None, None)),
        check_vma=False,
    )
```

```python
import jax
import jax.numpy as jnp
from jax import lax
from jax.sharding import PartitionSpec as P

D = 1600
HD = 64
PRIOR = 768
PAGE = 128
POOL = 12


EPSILON = 1e-05

GX_CORE = (1, 2)
GX_Y = (2, 4)
GX_XLO = (8, 2)
GY_XHI = (1, 2)
GY_Z = (2, 4)


def shift_pairs(count, stride, size, step):
    pairs = []
    for i in range(count):
        c = (i // stride) % size
        j = i + (((c + step) % size) - c) * stride
        if j != i:
            pairs.append((i, j))
    return pairs


def sub_gather(block, axis, sub):
    stride, size = sub
    count = lax.axis_size(axis)
    c = (lax.axis_index(axis) // stride) % size
    if size == 2:
        other = lax.ppermute(block, axis, shift_pairs(count, stride, size, 1))
        got = jnp.stack([block, other])
    else:
        from_left = lax.ppermute(block, axis, shift_pairs(count, stride, size, 1))
        from_right = lax.ppermute(block, axis, shift_pairs(count, stride, size, -1))
        from_two = lax.ppermute(from_left, axis, shift_pairs(count, stride, size, 1))
        got = jnp.stack([block, from_left, from_two, from_right])
    order = (c - jnp.arange(size, dtype=jnp.int32)) % size
    return jnp.take(got, order, axis=0)


def gather_gx(block):
    g = sub_gather(block, "gx", GX_CORE)
    g = sub_gather(g, "gx", GX_XLO)
    g = sub_gather(g, "gx", GX_Y)
    g = jnp.swapaxes(g, 0, 1)
    return g.reshape((-1,) + block.shape)


def gather_gy(block):
    g = sub_gather(block, "gy", GY_XHI)
    g = sub_gather(g, "gy", GY_Z)
    return g.reshape((-1,) + block.shape)


def reduce_scatter_gy(blocks):
    count = lax.axis_size("gy")
    idx = lax.axis_index("gy")
    z = idx // 2
    h = idx % 2
    zsize = GY_Z[1]
    by_z = blocks.reshape((zsize, 2) + blocks.shape[1:])
    total = lax.dynamic_index_in_dim(by_z, z, 0, keepdims=False)
    for step in range(1, zsize):
        outgoing = lax.dynamic_index_in_dim(by_z, (z + step) % zsize, 0, keepdims=False)
        arrived = lax.ppermute(
            outgoing.astype(jnp.bfloat16), "gy", shift_pairs(count, GY_Z[0], zsize, step)
        )
        total = total + arrived.astype(jnp.float32)
    keep = lax.dynamic_index_in_dim(total, h, 0, keepdims=False)
    give = lax.dynamic_index_in_dim(total, 1 - h, 0, keepdims=False)
    arrived = lax.ppermute(give.astype(jnp.bfloat16), "gy", shift_pairs(count, 1, 2, 1))
    return keep + arrived.astype(jnp.float32)


def finish_norm(row_block, row_sum, row_squares):
    average = row_sum / D
    variance = row_squares / D - average * average
    return (row_block - average) * lax.rsqrt(variance + EPSILON)


def normalized(row_block):
    return finish_norm(
        row_block,
        jnp.sum(row_block, axis=1, keepdims=True),
        jnp.sum(row_block * row_block, axis=1, keepdims=True),
    )


def ordered(own_part, other_part, is_first):
    lower_part = jnp.where(is_first, own_part, other_part)
    upper_part = jnp.where(is_first, other_part, own_part)
    return jnp.concatenate([lower_part, upper_part], axis=0)


def hand_over(kv_cache, prompt_group, page_table):
    moved_pages = lax.all_to_all(kv_cache, "gx", split_axis=0, concat_axis=2, tiled=True)
    columns = moved_pages.shape[3]
    pages_each = PRIOR // PAGE
    total_pages = moved_pages.shape[2] // PAGE
    groups = lax.axis_size("gy")
    page_ids = jnp.arange(total_pages, dtype=jnp.int32)
    destination = prompt_group[page_ids // pages_each] * POOL + page_table.reshape(-1)
    source = jnp.full((groups * POOL,), -1, jnp.int32).at[destination].set(page_ids)
    page_blocks = moved_pages.reshape(2, total_pages, PAGE * columns)
    chooser = (source[:, None] == page_ids[None, :]).astype(page_blocks.dtype)
    picked = jnp.einsum(
        "sp,cpf->csf", chooser, page_blocks, preferred_element_type=jnp.float32
    ).astype(page_blocks.dtype)
    picked = picked.reshape(2, groups, POOL * PAGE, columns)
    arrived = lax.all_to_all(picked, "gy", split_axis=1, concat_axis=1, tiled=True)
    arrived = arrived.transpose(0, 2, 1, 3)
    return arrived.reshape(1, 1, 2, POOL * PAGE, columns * groups)


def on_device(
    hidden,
    lengths,
    query_weight,
    key_weight,
    value_weight,
    out_weight,
    expand_weight,
    contract_weight,
    kv_cache,
    prompt_group,
    page_table,
):
    slot_count = hidden.shape[0]
    device_row = lax.axis_index("gx")
    is_first = device_row % 2 == 0
    prompt = device_row // 2
    offset = device_row % 2 * slot_count
    local_cols = query_weight.shape[1]

    qkv_block = jnp.concatenate([query_weight, key_weight, value_weight], axis=1)
    qkv_full = gather_gx(qkv_block).reshape(D, 3 * local_cols)
    query_full = qkv_full[:, :local_cols]
    key_full = qkv_full[:, local_cols : 2 * local_cols]
    value_full = qkv_full[:, 2 * local_cols :]

    ffn_block = jnp.concatenate([expand_weight, contract_weight.T], axis=1)
    qkv_full, ffn_block, out_weight = lax.optimization_barrier((qkv_full, ffn_block, out_weight))

    out_cols = jnp.moveaxis(gather_gx(out_weight), 0, 1).reshape(out_weight.shape[0], D)
    out_full = gather_gy(out_cols).reshape(-1, D)

    ffn_full = gather_gx(ffn_block).reshape(D, -1)
    ff_cols = expand_weight.shape[1]
    expand_full = ffn_full[:, :ff_cols]
    contract_full_t = ffn_full[:, ff_cols:]

    rows_full = hidden.astype(jnp.float32)
    normed = normalized(rows_full).astype(jnp.bfloat16)
    queries = jnp.dot(normed, query_full, preferred_element_type=jnp.float32)
    new_keys = jnp.dot(normed, key_full, preferred_element_type=jnp.float32).astype(jnp.bfloat16)
    new_values = jnp.dot(normed, value_full, preferred_element_type=jnp.float32).astype(
        jnp.bfloat16
    )
    prior_keys = kv_cache[0, 0]
    prior_values = kv_cache[0, 1]
    partner = lax.ppermute(
        (new_keys, new_values, prior_keys, prior_values),
        "gx",
        shift_pairs(lax.axis_size("gx"), 1, 2, 1),
    )
    all_keys = jnp.concatenate(
        [ordered(prior_keys, partner[2], is_first), ordered(new_keys, partner[0], is_first)], axis=0
    )
    all_values = jnp.concatenate(
        [ordered(prior_values, partner[3], is_first), ordered(new_values, partner[1], is_first)],
        axis=0,
    )
    prior_count = 2 * prior_keys.shape[0]
    query_pos = offset + jnp.arange(slot_count, dtype=jnp.int32)
    key_pos = jnp.arange(2 * slot_count, dtype=jnp.int32)
    allowed = jnp.concatenate(
        [jnp.ones((slot_count, prior_count), dtype=bool), key_pos[None, :] <= query_pos[:, None]],
        axis=1,
    )
    local_heads = queries.shape[1] // HD

    def split_heads(matrix):
        return matrix.reshape(matrix.shape[0], local_heads, HD).transpose(1, 0, 2)

    def one_head(operands):
        query_head, key_head, value_head = operands
        scores = jnp.einsum(
            "sd,kd->sk", query_head, key_head.astype(jnp.float32), precision=lax.Precision.HIGHEST
        ) * HD ** (-0.5)
        scores = jnp.where(allowed, scores, -jnp.inf)
        highest = jnp.max(scores, axis=1, keepdims=True)
        weights = jnp.exp(scores - highest)
        weight_sum = jnp.sum(weights, axis=1, keepdims=True)
        mixed_rows = jnp.dot(
            weights.astype(jnp.bfloat16), value_head, preferred_element_type=jnp.float32
        )
        return mixed_rows / weight_sum

    attended = lax.map(
        one_head, (split_heads(queries), split_heads(all_keys), split_heads(all_values))
    )
    attended = (
        attended.transpose(1, 0, 2).reshape(slot_count, local_heads * HD).astype(jnp.bfloat16)
    )
    attended_all = gather_gy(attended)
    attended_all = jnp.moveaxis(attended_all, 0, 1).reshape(slot_count, -1)
    residual = rows_full + jnp.dot(attended_all, out_full, preferred_element_type=jnp.float32)
    normed_two = normalized(residual).astype(jnp.bfloat16)
    expanded = jax.nn.gelu(
        jnp.dot(normed_two, expand_full, preferred_element_type=jnp.float32), approximate=True
    ).astype(jnp.bfloat16)
    contracted = lax.dot_general(
        expanded, contract_full_t, (((1,), (1,)), ((), ())), preferred_element_type=jnp.float32
    )
    groups = lax.axis_size("gy")
    own_width = D // groups
    blocks = contracted.reshape(slot_count, groups, own_width).transpose(1, 0, 2)
    summed = reduce_scatter_gy(blocks)
    column_start = lax.axis_index("gy") * own_width
    residual_own = lax.dynamic_slice_in_dim(residual, column_start, own_width, 1)
    is_valid = query_pos < lengths[prompt]
    output = jnp.where(is_valid[:, None], residual_own + summed, 0.0).astype(jnp.bfloat16)
    return (output, hand_over(kv_cache, prompt_group, page_table))


def solution(mesh):
    placed = (
        P("gx", None),
        P(),
        P("gx", "gy"),
        P("gx", "gy"),
        P("gx", "gy"),
        P("gy", "gx"),
        P("gx", "gy"),
        P("gy", "gx"),
        P(None, None, "gx", "gy"),
        P(),
        P(),
    )
    return jax.shard_map(
        on_device,
        mesh=mesh,
        in_specs=placed,
        out_specs=(P("gx", "gy"), P("gx", "gy", None, None, None)),
        check_vma=False,
    )
```

```python
import jax
import jax.numpy as jnp
from jax import lax
from jax.sharding import PartitionSpec as P

D = 1600
HD = 64
PRIOR = 768
PAGE = 128
POOL = 12


EPSILON = 1e-05

GX_CORE = (1, 2)
GX_Y = (2, 4)
GX_XLO = (8, 2)
GY_XHI = (1, 2)
GY_Z = (2, 4)


def shift_pairs(count, stride, size, step):
    pairs = []
    for i in range(count):
        c = (i // stride) % size
        j = i + (((c + step) % size) - c) * stride
        if j != i:
            pairs.append((i, j))
    return pairs


def sub_gather(block, axis, sub):
    stride, size = sub
    count = lax.axis_size(axis)
    c = (lax.axis_index(axis) // stride) % size
    if size == 2:
        other = lax.ppermute(block, axis, shift_pairs(count, stride, size, 1))
        got = jnp.stack([block, other])
    else:
        from_left = lax.ppermute(block, axis, shift_pairs(count, stride, size, 1))
        from_right = lax.ppermute(block, axis, shift_pairs(count, stride, size, -1))
        from_two = lax.ppermute(from_left, axis, shift_pairs(count, stride, size, 1))
        got = jnp.stack([block, from_left, from_two, from_right])
    order = (c - jnp.arange(size, dtype=jnp.int32)) % size
    return jnp.take(got, order, axis=0)


def gather_gx(block):
    g = sub_gather(block, "gx", GX_CORE)
    g = sub_gather(g, "gx", GX_XLO)
    g = sub_gather(g, "gx", GX_Y)
    g = jnp.swapaxes(g, 0, 1)
    return g.reshape((-1,) + block.shape)


def gather_gy(block):
    g = sub_gather(block, "gy", GY_XHI)
    g = sub_gather(g, "gy", GY_Z)
    return g.reshape((-1,) + block.shape)


def reduce_scatter_gy(blocks):
    count = lax.axis_size("gy")
    idx = lax.axis_index("gy")
    z = idx // 2
    h = idx % 2
    zsize = GY_Z[1]
    by_z = blocks.reshape((zsize, 2) + blocks.shape[1:])
    total = lax.dynamic_index_in_dim(by_z, z, 0, keepdims=False)
    for step in range(1, zsize):
        outgoing = lax.dynamic_index_in_dim(by_z, (z + step) % zsize, 0, keepdims=False)
        arrived = lax.ppermute(
            outgoing.astype(jnp.bfloat16), "gy", shift_pairs(count, GY_Z[0], zsize, step)
        )
        total = total + arrived.astype(jnp.float32)
    keep = lax.dynamic_index_in_dim(total, h, 0, keepdims=False)
    give = lax.dynamic_index_in_dim(total, 1 - h, 0, keepdims=False)
    arrived = lax.ppermute(give.astype(jnp.bfloat16), "gy", shift_pairs(count, 1, 2, 1))
    return keep + arrived.astype(jnp.float32)


def finish_norm(row_block, row_sum, row_squares):
    average = row_sum / D
    variance = row_squares / D - average * average
    return (row_block - average) * lax.rsqrt(variance + EPSILON)


def normalized(row_block):
    return finish_norm(
        row_block,
        jnp.sum(row_block, axis=1, keepdims=True),
        jnp.sum(row_block * row_block, axis=1, keepdims=True),
    )


def ordered(own_part, other_part, is_first):
    lower_part = jnp.where(is_first, own_part, other_part)
    upper_part = jnp.where(is_first, other_part, own_part)
    return jnp.concatenate([lower_part, upper_part], axis=0)


def hand_over_layers(kv_cache):
    return lax.all_to_all(kv_cache, "gx", split_axis=0, concat_axis=2, tiled=True)


def hand_over(moved_pages, prompt_group, page_table):
    columns = moved_pages.shape[3]
    pages_each = PRIOR // PAGE
    total_pages = moved_pages.shape[2] // PAGE
    groups = lax.axis_size("gy")
    page_ids = jnp.arange(total_pages, dtype=jnp.int32)
    destination = prompt_group[page_ids // pages_each] * POOL + page_table.reshape(-1)
    source = jnp.full((groups * POOL,), -1, jnp.int32).at[destination].set(page_ids)
    page_blocks = moved_pages.reshape(2, total_pages, PAGE, columns)
    picked = jnp.take(page_blocks, jnp.maximum(source, 0), axis=1)
    picked = jnp.where((source >= 0)[None, :, None, None], picked, jnp.zeros((), picked.dtype))
    picked = picked.reshape(2, groups, POOL * PAGE, columns)
    arrived = lax.all_to_all(picked, "gy", split_axis=1, concat_axis=1, tiled=True)
    arrived = jnp.concatenate([arrived[:, k] for k in range(groups)], axis=-1)
    return arrived.reshape(1, 1, 2, POOL * PAGE, columns * groups)


def on_device(
    hidden,
    lengths,
    query_weight,
    key_weight,
    value_weight,
    out_weight,
    expand_weight,
    contract_weight,
    kv_cache,
    prompt_group,
    page_table,
):
    slot_count = hidden.shape[0]
    device_row = lax.axis_index("gx")
    is_first = device_row % 2 == 0
    prompt = device_row // 2
    offset = device_row % 2 * slot_count
    local_cols = query_weight.shape[1]

    qkv_block = jnp.concatenate([query_weight, key_weight, value_weight], axis=1)
    qkv_full = gather_gx(qkv_block).reshape(D, 3 * local_cols)
    query_full = qkv_full[:, :local_cols]
    key_full = qkv_full[:, local_cols : 2 * local_cols]
    value_full = qkv_full[:, 2 * local_cols :]

    ffn_block = jnp.concatenate([expand_weight, contract_weight.T], axis=1)
    moved_pages = hand_over_layers(kv_cache)
    qkv_full, ffn_block, moved_pages = lax.optimization_barrier((qkv_full, ffn_block, moved_pages))

    out_cols = jnp.moveaxis(gather_gx(out_weight), 0, 1).reshape(out_weight.shape[0], D)
    out_full = gather_gy(out_cols).reshape(-1, D)

    ffn_full = gather_gx(ffn_block).reshape(D, -1)
    ff_cols = expand_weight.shape[1]
    expand_full = ffn_full[:, :ff_cols]
    contract_full_t = ffn_full[:, ff_cols:]

    rows_full = hidden.astype(jnp.float32)
    normed = normalized(rows_full).astype(jnp.bfloat16)
    queries = jnp.dot(normed, query_full, preferred_element_type=jnp.float32)
    new_keys = jnp.dot(normed, key_full, preferred_element_type=jnp.float32).astype(jnp.bfloat16)
    new_values = jnp.dot(normed, value_full, preferred_element_type=jnp.float32).astype(
        jnp.bfloat16
    )
    prior_keys = kv_cache[0, 0]
    prior_values = kv_cache[0, 1]
    partner = lax.ppermute(
        (new_keys, new_values, prior_keys, prior_values),
        "gx",
        shift_pairs(lax.axis_size("gx"), 1, 2, 1),
    )
    all_keys = jnp.concatenate(
        [ordered(prior_keys, partner[2], is_first), ordered(new_keys, partner[0], is_first)], axis=0
    )
    all_values = jnp.concatenate(
        [ordered(prior_values, partner[3], is_first), ordered(new_values, partner[1], is_first)],
        axis=0,
    )
    prior_count = 2 * prior_keys.shape[0]
    query_pos = offset + jnp.arange(slot_count, dtype=jnp.int32)
    key_pos = jnp.arange(2 * slot_count, dtype=jnp.int32)
    allowed = jnp.concatenate(
        [jnp.ones((slot_count, prior_count), dtype=bool), key_pos[None, :] <= query_pos[:, None]],
        axis=1,
    )
    local_heads = queries.shape[1] // HD

    def split_heads(matrix):
        return matrix.reshape(matrix.shape[0], local_heads, HD).transpose(1, 0, 2)

    def one_head(operands):
        query_head, key_head, value_head = operands
        scores = jnp.einsum(
            "sd,kd->sk", query_head, key_head.astype(jnp.float32), precision=lax.Precision.HIGHEST
        ) * HD ** (-0.5)
        scores = jnp.where(allowed, scores, -jnp.inf)
        highest = jnp.max(scores, axis=1, keepdims=True)
        weights = jnp.exp(scores - highest)
        weight_sum = jnp.sum(weights, axis=1, keepdims=True)
        mixed_rows = jnp.dot(
            weights.astype(jnp.bfloat16), value_head, preferred_element_type=jnp.float32
        )
        return mixed_rows / weight_sum

    attended = lax.map(
        one_head, (split_heads(queries), split_heads(all_keys), split_heads(all_values))
    )
    attended = (
        attended.transpose(1, 0, 2).reshape(slot_count, local_heads * HD).astype(jnp.bfloat16)
    )
    attended_all = gather_gy(attended)
    attended_all = jnp.moveaxis(attended_all, 0, 1).reshape(slot_count, -1)
    residual = rows_full + jnp.dot(attended_all, out_full, preferred_element_type=jnp.float32)
    normed_two = normalized(residual).astype(jnp.bfloat16)
    expanded = jax.nn.gelu(
        jnp.dot(normed_two, expand_full, preferred_element_type=jnp.float32), approximate=True
    ).astype(jnp.bfloat16)
    contracted = lax.dot_general(
        expanded, contract_full_t, (((1,), (1,)), ((), ())), preferred_element_type=jnp.float32
    )
    groups = lax.axis_size("gy")
    own_width = D // groups
    blocks = contracted.reshape(slot_count, groups, own_width).transpose(1, 0, 2)
    summed = reduce_scatter_gy(blocks)
    column_start = lax.axis_index("gy") * own_width
    residual_own = lax.dynamic_slice_in_dim(residual, column_start, own_width, 1)
    is_valid = query_pos < lengths[prompt]
    output = jnp.where(is_valid[:, None], residual_own + summed, 0.0).astype(jnp.bfloat16)
    return (output, hand_over(moved_pages, prompt_group, page_table))


def solution(mesh):
    placed = (
        P("gx", None),
        P(),
        P("gx", "gy"),
        P("gx", "gy"),
        P("gx", "gy"),
        P("gy", "gx"),
        P("gx", "gy"),
        P("gy", "gx"),
        P(None, None, "gx", "gy"),
        P(),
        P(),
    )
    return jax.shard_map(
        on_device,
        mesh=mesh,
        in_specs=placed,
        out_specs=(P("gx", "gy"), P("gx", "gy", None, None, None)),
        check_vma=False,
    )
```

```python
import jax
import jax.numpy as jnp
from jax import lax
from jax.sharding import PartitionSpec as P

D = 1600
HD = 64
PRIOR = 768
PAGE = 128
POOL = 12


EPSILON = 1e-05

GX_CORE = (1, 2)
GX_Y = (2, 4)
GX_XLO = (8, 2)
GY_XHI = (1, 2)
GY_Z = (2, 4)


def shift_pairs(count, stride, size, step):
    pairs = []
    for i in range(count):
        c = (i // stride) % size
        j = i + (((c + step) % size) - c) * stride
        if j != i:
            pairs.append((i, j))
    return pairs


def sub_gather(block, axis, sub):
    stride, size = sub
    count = lax.axis_size(axis)
    c = (lax.axis_index(axis) // stride) % size
    if size == 2:
        other = lax.ppermute(block, axis, shift_pairs(count, stride, size, 1))
        got = jnp.stack([block, other])
    else:
        from_left = lax.ppermute(block, axis, shift_pairs(count, stride, size, 1))
        from_right = lax.ppermute(block, axis, shift_pairs(count, stride, size, -1))
        from_two = lax.ppermute(from_left, axis, shift_pairs(count, stride, size, 1))
        got = jnp.stack([block, from_left, from_two, from_right])
    order = (c - jnp.arange(size, dtype=jnp.int32)) % size
    return jnp.take(got, order, axis=0)


def gather_gx(block):
    g = sub_gather(block, "gx", GX_XLO)
    g = sub_gather(g, "gx", GX_Y)
    g = sub_gather(g, "gx", GX_CORE)
    g = jnp.transpose(g, (2, 1, 0) + tuple(range(3, g.ndim)))
    return g.reshape((-1,) + block.shape)


def gather_gy(block):
    g = sub_gather(block, "gy", GY_XHI)
    g = sub_gather(g, "gy", GY_Z)
    return g.reshape((-1,) + block.shape)


def reduce_scatter_gy(blocks):
    count = lax.axis_size("gy")
    idx = lax.axis_index("gy")
    z = idx // 2
    h = idx % 2
    zsize = GY_Z[1]
    by_z = blocks.reshape((zsize, 2) + blocks.shape[1:])
    total = lax.dynamic_index_in_dim(by_z, z, 0, keepdims=False)
    for step in range(1, zsize):
        outgoing = lax.dynamic_index_in_dim(by_z, (z + step) % zsize, 0, keepdims=False)
        arrived = lax.ppermute(
            outgoing.astype(jnp.bfloat16), "gy", shift_pairs(count, GY_Z[0], zsize, step)
        )
        total = total + arrived.astype(jnp.float32)
    keep = lax.dynamic_index_in_dim(total, h, 0, keepdims=False)
    give = lax.dynamic_index_in_dim(total, 1 - h, 0, keepdims=False)
    arrived = lax.ppermute(give.astype(jnp.bfloat16), "gy", shift_pairs(count, 1, 2, 1))
    return keep + arrived.astype(jnp.float32)


def finish_norm(row_block, row_sum, row_squares):
    average = row_sum / D
    variance = row_squares / D - average * average
    return (row_block - average) * lax.rsqrt(variance + EPSILON)


def normalized(row_block):
    return finish_norm(
        row_block,
        jnp.sum(row_block, axis=1, keepdims=True),
        jnp.sum(row_block * row_block, axis=1, keepdims=True),
    )


def ordered(own_part, other_part, is_first):
    lower_part = jnp.where(is_first, own_part, other_part)
    upper_part = jnp.where(is_first, other_part, own_part)
    return jnp.concatenate([lower_part, upper_part], axis=0)


def hand_over(kv_cache, prompt_group, page_table):
    moved_pages = lax.all_to_all(kv_cache, "gx", split_axis=0, concat_axis=2, tiled=True)
    columns = moved_pages.shape[3]
    pages_each = PRIOR // PAGE
    total_pages = moved_pages.shape[2] // PAGE
    groups = lax.axis_size("gy")
    page_ids = jnp.arange(total_pages, dtype=jnp.int32)
    destination = prompt_group[page_ids // pages_each] * POOL + page_table.reshape(-1)
    source = jnp.full((groups * POOL,), -1, jnp.int32).at[destination].set(page_ids)
    page_blocks = moved_pages.reshape(2, total_pages, PAGE, columns)
    picked = jnp.take(page_blocks, jnp.maximum(source, 0), axis=1)
    picked = jnp.where((source >= 0)[None, :, None, None], picked, jnp.zeros((), picked.dtype))
    picked = picked.reshape(2, groups, POOL * PAGE, columns)
    arrived = lax.all_to_all(picked, "gy", split_axis=1, concat_axis=1, tiled=True)
    arrived = arrived.transpose(0, 2, 1, 3)
    return arrived.reshape(1, 1, 2, POOL * PAGE, columns * groups)


def on_device(
    hidden,
    lengths,
    query_weight,
    key_weight,
    value_weight,
    out_weight,
    expand_weight,
    contract_weight,
    kv_cache,
    prompt_group,
    page_table,
):
    slot_count = hidden.shape[0]
    device_row = lax.axis_index("gx")
    is_first = device_row % 2 == 0
    prompt = device_row // 2
    offset = device_row % 2 * slot_count
    local_cols = query_weight.shape[1]

    qkv_block = jnp.concatenate([query_weight, key_weight, value_weight], axis=1)
    qkv_full = gather_gx(qkv_block).reshape(D, 3 * local_cols)
    query_full = qkv_full[:, :local_cols]
    key_full = qkv_full[:, local_cols : 2 * local_cols]
    value_full = qkv_full[:, 2 * local_cols :]

    ffn_block = jnp.concatenate([expand_weight, contract_weight.T], axis=1)
    qkv_full, ffn_block, kv_cache = lax.optimization_barrier((qkv_full, ffn_block, kv_cache))

    out_rows = gather_gy(out_weight).reshape(-1, out_weight.shape[1])
    out_full = jnp.moveaxis(gather_gx(out_rows), 0, 1).reshape(out_rows.shape[0], D)

    ffn_full = gather_gx(ffn_block).reshape(D, -1)
    ff_cols = expand_weight.shape[1]
    expand_full = ffn_full[:, :ff_cols]
    contract_full_t = ffn_full[:, ff_cols:]

    rows_full = hidden.astype(jnp.float32)
    normed = normalized(rows_full).astype(jnp.bfloat16)
    queries = jnp.dot(normed, query_full, preferred_element_type=jnp.float32)
    new_keys = jnp.dot(normed, key_full, preferred_element_type=jnp.float32).astype(jnp.bfloat16)
    new_values = jnp.dot(normed, value_full, preferred_element_type=jnp.float32).astype(
        jnp.bfloat16
    )
    prior_keys = kv_cache[0, 0]
    prior_values = kv_cache[0, 1]
    partner = lax.ppermute(
        (new_keys, new_values, prior_keys, prior_values),
        "gx",
        shift_pairs(lax.axis_size("gx"), 1, 2, 1),
    )
    all_keys = jnp.concatenate(
        [ordered(prior_keys, partner[2], is_first), ordered(new_keys, partner[0], is_first)], axis=0
    )
    all_values = jnp.concatenate(
        [ordered(prior_values, partner[3], is_first), ordered(new_values, partner[1], is_first)],
        axis=0,
    )
    prior_count = 2 * prior_keys.shape[0]
    query_pos = offset + jnp.arange(slot_count, dtype=jnp.int32)
    key_pos = jnp.arange(2 * slot_count, dtype=jnp.int32)
    allowed = jnp.concatenate(
        [jnp.ones((slot_count, prior_count), dtype=bool), key_pos[None, :] <= query_pos[:, None]],
        axis=1,
    )
    local_heads = queries.shape[1] // HD

    def split_heads(matrix):
        return matrix.reshape(matrix.shape[0], local_heads, HD).transpose(1, 0, 2)

    def one_head(operands):
        query_head, key_head, value_head = operands
        scores = jnp.einsum(
            "sd,kd->sk", query_head, key_head.astype(jnp.float32), precision=lax.Precision.HIGHEST
        ) * HD ** (-0.5)
        scores = jnp.where(allowed, scores, -jnp.inf)
        highest = jnp.max(scores, axis=1, keepdims=True)
        weights = jnp.exp(scores - highest)
        weight_sum = jnp.sum(weights, axis=1, keepdims=True)
        mixed_rows = jnp.dot(
            weights.astype(jnp.bfloat16), value_head, preferred_element_type=jnp.float32
        )
        return mixed_rows / weight_sum

    attended = lax.map(
        one_head, (split_heads(queries), split_heads(all_keys), split_heads(all_values))
    )
    attended = (
        attended.transpose(1, 0, 2).reshape(slot_count, local_heads * HD).astype(jnp.bfloat16)
    )
    attended_all = gather_gy(attended)
    attended_all = jnp.moveaxis(attended_all, 0, 1).reshape(slot_count, -1)
    residual = rows_full + jnp.dot(attended_all, out_full, preferred_element_type=jnp.float32)
    normed_two = normalized(residual).astype(jnp.bfloat16)
    expanded = jax.nn.gelu(
        jnp.dot(normed_two, expand_full, preferred_element_type=jnp.float32), approximate=True
    ).astype(jnp.bfloat16)
    contracted = lax.dot_general(
        expanded, contract_full_t, (((1,), (1,)), ((), ())), preferred_element_type=jnp.float32
    )
    groups = lax.axis_size("gy")
    own_width = D // groups
    blocks = contracted.reshape(slot_count, groups, own_width).transpose(1, 0, 2)
    summed = reduce_scatter_gy(blocks)
    column_start = lax.axis_index("gy") * own_width
    residual_own = lax.dynamic_slice_in_dim(residual, column_start, own_width, 1)
    is_valid = query_pos < lengths[prompt]
    output = jnp.where(is_valid[:, None], residual_own + summed, 0.0).astype(jnp.bfloat16)
    return (output, hand_over(kv_cache, prompt_group, page_table))


def solution(mesh):
    placed = (
        P("gx", None),
        P(),
        P("gx", "gy"),
        P("gx", "gy"),
        P("gx", "gy"),
        P("gy", "gx"),
        P("gx", "gy"),
        P("gy", "gx"),
        P(None, None, "gx", "gy"),
        P(),
        P(),
    )
    return jax.shard_map(
        on_device,
        mesh=mesh,
        in_specs=placed,
        out_specs=(P("gx", "gy"), P("gx", "gy", None, None, None)),
        check_vma=False,
    )
```

```python
import jax
import jax.numpy as jnp
from jax import lax
from jax.sharding import PartitionSpec as P

D = 1600
HD = 64
PRIOR = 768
PAGE = 128
POOL = 12


EPSILON = 1e-05

GX_CORE = (1, 2)
GX_Y = (2, 4)
GX_XLO = (8, 2)
GY_XHI = (1, 2)
GY_Z = (2, 4)


def shift_pairs(count, stride, size, step):
    pairs = []
    for i in range(count):
        c = (i // stride) % size
        j = i + (((c + step) % size) - c) * stride
        if j != i:
            pairs.append((i, j))
    return pairs


def sub_gather(block, axis, sub):
    stride, size = sub
    count = lax.axis_size(axis)
    c = (lax.axis_index(axis) // stride) % size
    if size == 2:
        other = lax.ppermute(block, axis, shift_pairs(count, stride, size, 1))
        got = jnp.stack([block, other])
    else:
        from_left = lax.ppermute(block, axis, shift_pairs(count, stride, size, 1))
        from_right = lax.ppermute(block, axis, shift_pairs(count, stride, size, -1))
        from_two = lax.ppermute(from_left, axis, shift_pairs(count, stride, size, 1))
        got = jnp.stack([block, from_left, from_two, from_right])
    order = (c - jnp.arange(size, dtype=jnp.int32)) % size
    return jnp.take(got, order, axis=0)


def gather_gx(block):
    g = sub_gather(block, "gx", GX_CORE)
    g = sub_gather(g, "gx", GX_XLO)
    g = sub_gather(g, "gx", GX_Y)
    g = jnp.swapaxes(g, 0, 1)
    return g.reshape((-1,) + block.shape)


def gather_gy(block):
    g = sub_gather(block, "gy", GY_XHI)
    g = sub_gather(g, "gy", GY_Z)
    return g.reshape((-1,) + block.shape)


def reduce_scatter_gy(blocks):
    count = lax.axis_size("gy")
    idx = lax.axis_index("gy")
    z = idx // 2
    h = idx % 2
    zsize = GY_Z[1]
    by_z = blocks.reshape((zsize, 2) + blocks.shape[1:])
    total = lax.dynamic_index_in_dim(by_z, z, 0, keepdims=False)
    for step in range(1, zsize):
        outgoing = lax.dynamic_index_in_dim(by_z, (z + step) % zsize, 0, keepdims=False)
        arrived = lax.ppermute(
            outgoing.astype(jnp.bfloat16), "gy", shift_pairs(count, GY_Z[0], zsize, step)
        )
        total = total + arrived.astype(jnp.float32)
    keep = lax.dynamic_index_in_dim(total, h, 0, keepdims=False)
    give = lax.dynamic_index_in_dim(total, 1 - h, 0, keepdims=False)
    arrived = lax.ppermute(give.astype(jnp.bfloat16), "gy", shift_pairs(count, 1, 2, 1))
    return keep + arrived.astype(jnp.float32)


def finish_norm(row_block, row_sum, row_squares):
    average = row_sum / D
    variance = row_squares / D - average * average
    return (row_block - average) * lax.rsqrt(variance + EPSILON)


def normalized(row_block):
    return finish_norm(
        row_block,
        jnp.sum(row_block, axis=1, keepdims=True),
        jnp.sum(row_block * row_block, axis=1, keepdims=True),
    )


def ordered(own_part, other_part, is_first):
    lower_part = jnp.where(is_first, own_part, other_part)
    upper_part = jnp.where(is_first, other_part, own_part)
    return jnp.concatenate([lower_part, upper_part], axis=0)


def sub_all_to_all(parts, axis, sub):
    stride, size = sub
    count = lax.axis_size(axis)
    c = (lax.axis_index(axis) // stride) % size
    got = [lax.dynamic_index_in_dim(parts, c, 0, keepdims=False)]
    for step in range(1, size):
        outgoing = lax.dynamic_index_in_dim(parts, (c + step) % size, 0, keepdims=False)
        got.append(lax.ppermute(outgoing, axis, shift_pairs(count, stride, size, step)))
    order = (c - jnp.arange(size, dtype=jnp.int32)) % size
    return jnp.take(jnp.stack(got), order, axis=0)


def layers_to_devices(kv_cache):
    rest = kv_cache.shape[1:]
    parts = kv_cache.reshape((GX_XLO[1], GX_Y[1], GX_CORE[1]) + rest)
    parts = sub_all_to_all(parts, "gx", GX_XLO)
    parts = sub_all_to_all(jnp.swapaxes(parts, 0, 1), "gx", GX_Y)
    parts = sub_all_to_all(jnp.moveaxis(parts, 2, 0), "gx", GX_CORE)
    parts = jnp.transpose(parts, (3, 2, 1, 0, 4, 5))
    return parts.reshape(rest[0], -1, rest[2])


def hand_over(kv_cache, prompt_group, page_table):
    moved_pages = layers_to_devices(kv_cache)[None]
    columns = moved_pages.shape[3]
    pages_each = PRIOR // PAGE
    total_pages = moved_pages.shape[2] // PAGE
    groups = lax.axis_size("gy")
    page_ids = jnp.arange(total_pages, dtype=jnp.int32)
    destination = prompt_group[page_ids // pages_each] * POOL + page_table.reshape(-1)
    source = jnp.full((groups * POOL,), -1, jnp.int32).at[destination].set(page_ids)
    page_blocks = moved_pages.reshape(2, total_pages, PAGE, columns)
    picked = jnp.take(page_blocks, jnp.maximum(source, 0), axis=1)
    picked = jnp.where((source >= 0)[None, :, None, None], picked, jnp.zeros((), picked.dtype))
    picked = picked.reshape(2, groups, POOL * PAGE, columns)
    arrived = lax.all_to_all(picked, "gy", split_axis=1, concat_axis=1, tiled=True)
    arrived = arrived.transpose(0, 2, 1, 3)
    return arrived.reshape(1, 1, 2, POOL * PAGE, columns * groups)


def on_device(
    hidden,
    lengths,
    query_weight,
    key_weight,
    value_weight,
    out_weight,
    expand_weight,
    contract_weight,
    kv_cache,
    prompt_group,
    page_table,
):
    slot_count = hidden.shape[0]
    device_row = lax.axis_index("gx")
    is_first = device_row % 2 == 0
    prompt = device_row // 2
    offset = device_row % 2 * slot_count
    local_cols = query_weight.shape[1]

    qkv_block = jnp.concatenate([query_weight, key_weight, value_weight], axis=1)
    qkv_full = gather_gx(qkv_block).reshape(D, 3 * local_cols)
    query_full = qkv_full[:, :local_cols]
    key_full = qkv_full[:, local_cols : 2 * local_cols]
    value_full = qkv_full[:, 2 * local_cols :]

    ffn_block = jnp.concatenate([expand_weight, contract_weight.T], axis=1)
    qkv_full, ffn_block, kv_cache = lax.optimization_barrier((qkv_full, ffn_block, kv_cache))

    out_cols = jnp.moveaxis(gather_gx(out_weight), 0, 1).reshape(out_weight.shape[0], D)
    out_full = gather_gy(out_cols).reshape(-1, D)

    ffn_full = gather_gx(ffn_block).reshape(D, -1)
    ff_cols = expand_weight.shape[1]
    expand_full = ffn_full[:, :ff_cols]
    contract_full_t = ffn_full[:, ff_cols:]

    rows_full = hidden.astype(jnp.float32)
    normed = normalized(rows_full).astype(jnp.bfloat16)
    queries = jnp.dot(normed, query_full, preferred_element_type=jnp.float32)
    new_keys = jnp.dot(normed, key_full, preferred_element_type=jnp.float32).astype(jnp.bfloat16)
    new_values = jnp.dot(normed, value_full, preferred_element_type=jnp.float32).astype(
        jnp.bfloat16
    )
    prior_keys = kv_cache[0, 0]
    prior_values = kv_cache[0, 1]
    partner = lax.ppermute(
        (new_keys, new_values, prior_keys, prior_values),
        "gx",
        shift_pairs(lax.axis_size("gx"), 1, 2, 1),
    )
    all_keys = jnp.concatenate(
        [ordered(prior_keys, partner[2], is_first), ordered(new_keys, partner[0], is_first)], axis=0
    )
    all_values = jnp.concatenate(
        [ordered(prior_values, partner[3], is_first), ordered(new_values, partner[1], is_first)],
        axis=0,
    )
    prior_count = 2 * prior_keys.shape[0]
    query_pos = offset + jnp.arange(slot_count, dtype=jnp.int32)
    key_pos = jnp.arange(2 * slot_count, dtype=jnp.int32)
    allowed = jnp.concatenate(
        [jnp.ones((slot_count, prior_count), dtype=bool), key_pos[None, :] <= query_pos[:, None]],
        axis=1,
    )
    local_heads = queries.shape[1] // HD

    def split_heads(matrix):
        return matrix.reshape(matrix.shape[0], local_heads, HD).transpose(1, 0, 2)

    def one_head(operands):
        query_head, key_head, value_head = operands
        scores = jnp.einsum(
            "sd,kd->sk", query_head, key_head.astype(jnp.float32), precision=lax.Precision.HIGHEST
        ) * HD ** (-0.5)
        scores = jnp.where(allowed, scores, -jnp.inf)
        highest = jnp.max(scores, axis=1, keepdims=True)
        weights = jnp.exp(scores - highest)
        weight_sum = jnp.sum(weights, axis=1, keepdims=True)
        mixed_rows = jnp.dot(
            weights.astype(jnp.bfloat16), value_head, preferred_element_type=jnp.float32
        )
        return mixed_rows / weight_sum

    attended = lax.map(
        one_head, (split_heads(queries), split_heads(all_keys), split_heads(all_values))
    )
    attended = (
        attended.transpose(1, 0, 2).reshape(slot_count, local_heads * HD).astype(jnp.bfloat16)
    )
    attended_all = gather_gy(attended)
    attended_all = jnp.moveaxis(attended_all, 0, 1).reshape(slot_count, -1)
    residual = rows_full + jnp.dot(attended_all, out_full, preferred_element_type=jnp.float32)
    normed_two = normalized(residual).astype(jnp.bfloat16)
    expanded = jax.nn.gelu(
        jnp.dot(normed_two, expand_full, preferred_element_type=jnp.float32), approximate=True
    ).astype(jnp.bfloat16)
    contracted = lax.dot_general(
        expanded, contract_full_t, (((1,), (1,)), ((), ())), preferred_element_type=jnp.float32
    )
    groups = lax.axis_size("gy")
    own_width = D // groups
    blocks = contracted.reshape(slot_count, groups, own_width).transpose(1, 0, 2)
    summed = reduce_scatter_gy(blocks)
    column_start = lax.axis_index("gy") * own_width
    residual_own = lax.dynamic_slice_in_dim(residual, column_start, own_width, 1)
    is_valid = query_pos < lengths[prompt]
    output = jnp.where(is_valid[:, None], residual_own + summed, 0.0).astype(jnp.bfloat16)
    return (output, hand_over(kv_cache, prompt_group, page_table))


def solution(mesh):
    placed = (
        P("gx", None),
        P(),
        P("gx", "gy"),
        P("gx", "gy"),
        P("gx", "gy"),
        P("gy", "gx"),
        P("gx", "gy"),
        P("gy", "gx"),
        P(None, None, "gx", "gy"),
        P(),
        P(),
    )
    return jax.shard_map(
        on_device,
        mesh=mesh,
        in_specs=placed,
        out_specs=(P("gx", "gy"), P("gx", "gy", None, None, None)),
        check_vma=False,
    )
```

```python
import jax
import jax.numpy as jnp
from jax import lax
from jax.sharding import PartitionSpec as P

D = 1600
HD = 64
PRIOR = 768
PAGE = 128
POOL = 12


EPSILON = 1e-05

GX_CORE = (1, 2)
GX_Y = (2, 4)
GX_XLO = (8, 2)
GY_XHI = (1, 2)
GY_Z = (2, 4)


def shift_pairs(count, stride, size, step):
    pairs = []
    for i in range(count):
        c = (i // stride) % size
        j = i + (((c + step) % size) - c) * stride
        if j != i:
            pairs.append((i, j))
    return pairs


def sub_gather(block, axis, sub):
    stride, size = sub
    count = lax.axis_size(axis)
    c = (lax.axis_index(axis) // stride) % size
    if size == 2:
        other = lax.ppermute(block, axis, shift_pairs(count, stride, size, 1))
        got = jnp.stack([block, other])
    else:
        from_left = lax.ppermute(block, axis, shift_pairs(count, stride, size, 1))
        from_right = lax.ppermute(block, axis, shift_pairs(count, stride, size, -1))
        from_two = lax.ppermute(from_left, axis, shift_pairs(count, stride, size, 1))
        got = jnp.stack([block, from_left, from_two, from_right])
    order = (c - jnp.arange(size, dtype=jnp.int32)) % size
    return jnp.take(got, order, axis=0)


def gather_gx(block):
    g = sub_gather(block, "gx", GX_CORE)
    g = sub_gather(g, "gx", GX_XLO)
    g = sub_gather(g, "gx", GX_Y)
    g = jnp.swapaxes(g, 0, 1)
    return g.reshape((-1,) + block.shape)


def gather_gy(block):
    g = sub_gather(block, "gy", GY_XHI)
    g = sub_gather(g, "gy", GY_Z)
    return g.reshape((-1,) + block.shape)


def reduce_scatter_gy(blocks):
    count = lax.axis_size("gy")
    idx = lax.axis_index("gy")
    z = idx // 2
    h = idx % 2
    zsize = GY_Z[1]
    by_z = blocks.reshape((zsize, 2) + blocks.shape[1:])
    total = lax.dynamic_index_in_dim(by_z, z, 0, keepdims=False)
    for step in range(1, zsize):
        outgoing = lax.dynamic_index_in_dim(by_z, (z + step) % zsize, 0, keepdims=False)
        arrived = lax.ppermute(
            outgoing.astype(jnp.bfloat16), "gy", shift_pairs(count, GY_Z[0], zsize, step)
        )
        total = total + arrived.astype(jnp.float32)
    keep = lax.dynamic_index_in_dim(total, h, 0, keepdims=False)
    give = lax.dynamic_index_in_dim(total, 1 - h, 0, keepdims=False)
    arrived = lax.ppermute(give.astype(jnp.bfloat16), "gy", shift_pairs(count, 1, 2, 1))
    return keep + arrived.astype(jnp.float32)


def a2a_gather(block, axis):
    count = lax.axis_size(axis)
    copies = jnp.broadcast_to(block[None], (count,) + block.shape)
    return lax.all_to_all(copies, axis, 0, 0, tiled=True)


def finish_norm(row_block, row_sum, row_squares):
    average = row_sum / D
    variance = row_squares / D - average * average
    return (row_block - average) * lax.rsqrt(variance + EPSILON)


def normalized(row_block):
    return finish_norm(
        row_block,
        jnp.sum(row_block, axis=1, keepdims=True),
        jnp.sum(row_block * row_block, axis=1, keepdims=True),
    )


def ordered(own_part, other_part, is_first):
    lower_part = jnp.where(is_first, own_part, other_part)
    upper_part = jnp.where(is_first, other_part, own_part)
    return jnp.concatenate([lower_part, upper_part], axis=0)


def hand_over(kv_cache, prompt_group, page_table):
    moved_pages = lax.all_to_all(kv_cache, "gx", split_axis=0, concat_axis=2, tiled=True)
    columns = moved_pages.shape[3]
    pages_each = PRIOR // PAGE
    total_pages = moved_pages.shape[2] // PAGE
    groups = lax.axis_size("gy")
    page_ids = jnp.arange(total_pages, dtype=jnp.int32)
    destination = prompt_group[page_ids // pages_each] * POOL + page_table.reshape(-1)
    source = jnp.full((groups * POOL,), -1, jnp.int32).at[destination].set(page_ids)
    page_blocks = moved_pages.reshape(2, total_pages, PAGE, columns)
    picked = jnp.take(page_blocks, jnp.maximum(source, 0), axis=1)
    picked = jnp.where((source >= 0)[None, :, None, None], picked, jnp.zeros((), picked.dtype))
    picked = picked.reshape(2, groups, POOL * PAGE, columns)
    arrived = lax.all_to_all(picked, "gy", split_axis=1, concat_axis=1, tiled=True)
    arrived = arrived.transpose(0, 2, 1, 3)
    return arrived.reshape(1, 1, 2, POOL * PAGE, columns * groups)


def on_device(
    hidden,
    lengths,
    query_weight,
    key_weight,
    value_weight,
    out_weight,
    expand_weight,
    contract_weight,
    kv_cache,
    prompt_group,
    page_table,
):
    slot_count = hidden.shape[0]
    device_row = lax.axis_index("gx")
    is_first = device_row % 2 == 0
    prompt = device_row // 2
    offset = device_row % 2 * slot_count
    local_cols = query_weight.shape[1]

    qkv_block = jnp.concatenate([query_weight, key_weight, value_weight], axis=1)
    qkv_full = a2a_gather(qkv_block, "gx").reshape(D, 3 * local_cols)
    query_full = qkv_full[:, :local_cols]
    key_full = qkv_full[:, local_cols : 2 * local_cols]
    value_full = qkv_full[:, 2 * local_cols :]

    ffn_block = jnp.concatenate([expand_weight, contract_weight.T], axis=1)
    qkv_full, ffn_block, kv_cache = lax.optimization_barrier((qkv_full, ffn_block, kv_cache))

    out_cols = jnp.moveaxis(gather_gx(out_weight), 0, 1).reshape(out_weight.shape[0], D)
    out_full = gather_gy(out_cols).reshape(-1, D)

    ffn_full = gather_gx(ffn_block).reshape(D, -1)
    ff_cols = expand_weight.shape[1]
    expand_full = ffn_full[:, :ff_cols]
    contract_full_t = ffn_full[:, ff_cols:]

    rows_full = hidden.astype(jnp.float32)
    normed = normalized(rows_full).astype(jnp.bfloat16)
    queries = jnp.dot(normed, query_full, preferred_element_type=jnp.float32)
    new_keys = jnp.dot(normed, key_full, preferred_element_type=jnp.float32).astype(jnp.bfloat16)
    new_values = jnp.dot(normed, value_full, preferred_element_type=jnp.float32).astype(
        jnp.bfloat16
    )
    prior_keys = kv_cache[0, 0]
    prior_values = kv_cache[0, 1]
    partner = lax.ppermute(
        (new_keys, new_values, prior_keys, prior_values),
        "gx",
        shift_pairs(lax.axis_size("gx"), 1, 2, 1),
    )
    all_keys = jnp.concatenate(
        [ordered(prior_keys, partner[2], is_first), ordered(new_keys, partner[0], is_first)], axis=0
    )
    all_values = jnp.concatenate(
        [ordered(prior_values, partner[3], is_first), ordered(new_values, partner[1], is_first)],
        axis=0,
    )
    prior_count = 2 * prior_keys.shape[0]
    query_pos = offset + jnp.arange(slot_count, dtype=jnp.int32)
    key_pos = jnp.arange(2 * slot_count, dtype=jnp.int32)
    allowed = jnp.concatenate(
        [jnp.ones((slot_count, prior_count), dtype=bool), key_pos[None, :] <= query_pos[:, None]],
        axis=1,
    )
    local_heads = queries.shape[1] // HD

    def split_heads(matrix):
        return matrix.reshape(matrix.shape[0], local_heads, HD).transpose(1, 0, 2)

    def one_head(operands):
        query_head, key_head, value_head = operands
        scores = jnp.einsum(
            "sd,kd->sk", query_head, key_head.astype(jnp.float32), precision=lax.Precision.HIGHEST
        ) * HD ** (-0.5)
        scores = jnp.where(allowed, scores, -jnp.inf)
        highest = jnp.max(scores, axis=1, keepdims=True)
        weights = jnp.exp(scores - highest)
        weight_sum = jnp.sum(weights, axis=1, keepdims=True)
        mixed_rows = jnp.dot(
            weights.astype(jnp.bfloat16), value_head, preferred_element_type=jnp.float32
        )
        return mixed_rows / weight_sum

    attended = lax.map(
        one_head, (split_heads(queries), split_heads(all_keys), split_heads(all_values))
    )
    attended = (
        attended.transpose(1, 0, 2).reshape(slot_count, local_heads * HD).astype(jnp.bfloat16)
    )
    attended_all = gather_gy(attended)
    attended_all = jnp.moveaxis(attended_all, 0, 1).reshape(slot_count, -1)
    residual = rows_full + jnp.dot(attended_all, out_full, preferred_element_type=jnp.float32)
    normed_two = normalized(residual).astype(jnp.bfloat16)
    expanded = jax.nn.gelu(
        jnp.dot(normed_two, expand_full, preferred_element_type=jnp.float32), approximate=True
    ).astype(jnp.bfloat16)
    contracted = lax.dot_general(
        expanded, contract_full_t, (((1,), (1,)), ((), ())), preferred_element_type=jnp.float32
    )
    groups = lax.axis_size("gy")
    own_width = D // groups
    blocks = contracted.reshape(slot_count, groups, own_width).transpose(1, 0, 2)
    summed = reduce_scatter_gy(blocks)
    column_start = lax.axis_index("gy") * own_width
    residual_own = lax.dynamic_slice_in_dim(residual, column_start, own_width, 1)
    is_valid = query_pos < lengths[prompt]
    output = jnp.where(is_valid[:, None], residual_own + summed, 0.0).astype(jnp.bfloat16)
    return (output, hand_over(kv_cache, prompt_group, page_table))


def solution(mesh):
    placed = (
        P("gx", None),
        P(),
        P("gx", "gy"),
        P("gx", "gy"),
        P("gx", "gy"),
        P("gy", "gx"),
        P("gx", "gy"),
        P("gy", "gx"),
        P(None, None, "gx", "gy"),
        P(),
        P(),
    )
    return jax.shard_map(
        on_device,
        mesh=mesh,
        in_specs=placed,
        out_specs=(P("gx", "gy"), P("gx", "gy", None, None, None)),
        check_vma=False,
    )
```

```python
import jax
import jax.numpy as jnp
from jax import lax
from jax.sharding import PartitionSpec as P

D = 1600
HD = 64
PRIOR = 768
PAGE = 128
POOL = 12


EPSILON = 1e-05

GX_CORE = (1, 2)
GX_Y = (2, 4)
GX_XLO = (8, 2)
GY_XHI = (1, 2)
GY_Z = (2, 4)


def shift_pairs(count, stride, size, step):
    pairs = []
    for i in range(count):
        c = (i // stride) % size
        j = i + (((c + step) % size) - c) * stride
        if j != i:
            pairs.append((i, j))
    return pairs


def sub_gather(block, axis, sub):
    stride, size = sub
    count = lax.axis_size(axis)
    c = (lax.axis_index(axis) // stride) % size
    if size == 2:
        other = lax.ppermute(block, axis, shift_pairs(count, stride, size, 1))
        got = jnp.stack([block, other])
    else:
        from_left = lax.ppermute(block, axis, shift_pairs(count, stride, size, 1))
        from_right = lax.ppermute(block, axis, shift_pairs(count, stride, size, -1))
        from_two = lax.ppermute(from_left, axis, shift_pairs(count, stride, size, 1))
        got = jnp.stack([block, from_left, from_two, from_right])
    order = (c - jnp.arange(size, dtype=jnp.int32)) % size
    return jnp.take(got, order, axis=0)


def gather_gx(block):
    g = sub_gather(block, "gx", GX_CORE)
    g = sub_gather(g, "gx", GX_XLO)
    g = sub_gather(g, "gx", GX_Y)
    g = jnp.swapaxes(g, 0, 1)
    return g.reshape((-1,) + block.shape)


def gather_gy(block):
    g = sub_gather(block, "gy", GY_XHI)
    g = sub_gather(g, "gy", GY_Z)
    return g.reshape((-1,) + block.shape)


def reduce_scatter_gy(blocks):
    count = lax.axis_size("gy")
    idx = lax.axis_index("gy")
    z = idx // 2
    h = idx % 2
    zsize = GY_Z[1]
    by_z = blocks.reshape((zsize, 2) + blocks.shape[1:])
    total = lax.dynamic_index_in_dim(by_z, z, 0, keepdims=False)
    for step in range(1, zsize):
        outgoing = lax.dynamic_index_in_dim(by_z, (z + step) % zsize, 0, keepdims=False)
        arrived = lax.ppermute(
            outgoing.astype(jnp.bfloat16), "gy", shift_pairs(count, GY_Z[0], zsize, step)
        )
        total = total + arrived.astype(jnp.float32)
    keep = lax.dynamic_index_in_dim(total, h, 0, keepdims=False)
    give = lax.dynamic_index_in_dim(total, 1 - h, 0, keepdims=False)
    arrived = lax.ppermute(give.astype(jnp.bfloat16), "gy", shift_pairs(count, 1, 2, 1))
    return keep + arrived.astype(jnp.float32)


def a2a_gather(block, axis):
    count = lax.axis_size(axis)
    copies = jnp.broadcast_to(block[None], (count,) + block.shape)
    return lax.all_to_all(copies, axis, 0, 0, tiled=True)


def finish_norm(row_block, row_sum, row_squares):
    average = row_sum / D
    variance = row_squares / D - average * average
    return (row_block - average) * lax.rsqrt(variance + EPSILON)


def normalized(row_block):
    return finish_norm(
        row_block,
        jnp.sum(row_block, axis=1, keepdims=True),
        jnp.sum(row_block * row_block, axis=1, keepdims=True),
    )


def ordered(own_part, other_part, is_first):
    lower_part = jnp.where(is_first, own_part, other_part)
    upper_part = jnp.where(is_first, other_part, own_part)
    return jnp.concatenate([lower_part, upper_part], axis=0)


def hand_over(kv_cache, prompt_group, page_table):
    moved_pages = lax.all_to_all(kv_cache, "gx", split_axis=0, concat_axis=2, tiled=True)
    columns = moved_pages.shape[3]
    pages_each = PRIOR // PAGE
    total_pages = moved_pages.shape[2] // PAGE
    groups = lax.axis_size("gy")
    page_ids = jnp.arange(total_pages, dtype=jnp.int32)
    destination = prompt_group[page_ids // pages_each] * POOL + page_table.reshape(-1)
    source = jnp.full((groups * POOL,), -1, jnp.int32).at[destination].set(page_ids)
    page_blocks = moved_pages.reshape(2, total_pages, PAGE, columns)
    picked = jnp.take(page_blocks, jnp.maximum(source, 0), axis=1)
    picked = jnp.where((source >= 0)[None, :, None, None], picked, jnp.zeros((), picked.dtype))
    picked = picked.reshape(2, groups, POOL * PAGE, columns)
    arrived = lax.all_to_all(picked, "gy", split_axis=1, concat_axis=1, tiled=True)
    arrived = jnp.concatenate([arrived[:, k] for k in range(groups)], axis=-1)
    return arrived.reshape(1, 1, 2, POOL * PAGE, columns * groups)


def on_device(
    hidden,
    lengths,
    query_weight,
    key_weight,
    value_weight,
    out_weight,
    expand_weight,
    contract_weight,
    kv_cache,
    prompt_group,
    page_table,
):
    slot_count = hidden.shape[0]
    device_row = lax.axis_index("gx")
    is_first = device_row % 2 == 0
    prompt = device_row // 2
    offset = device_row % 2 * slot_count
    local_cols = query_weight.shape[1]

    qkv_block = jnp.concatenate([query_weight, key_weight, value_weight], axis=1)
    qkv_full = a2a_gather(qkv_block, "gx").reshape(D, 3 * local_cols)
    query_full = qkv_full[:, :local_cols]
    key_full = qkv_full[:, local_cols : 2 * local_cols]
    value_full = qkv_full[:, 2 * local_cols :]

    ffn_block = jnp.concatenate([expand_weight, contract_weight.T], axis=1)
    qkv_full, ffn_block, kv_cache, out_weight = lax.optimization_barrier(
        (qkv_full, ffn_block, kv_cache, out_weight)
    )

    out_cols = jnp.moveaxis(gather_gx(out_weight), 0, 1).reshape(out_weight.shape[0], D)
    out_full = gather_gy(out_cols).reshape(-1, D)

    ffn_full = gather_gx(ffn_block).reshape(D, -1)
    ff_cols = expand_weight.shape[1]
    expand_full = ffn_full[:, :ff_cols]
    contract_full_t = ffn_full[:, ff_cols:]

    rows_full = hidden.astype(jnp.float32)
    normed = normalized(rows_full).astype(jnp.bfloat16)
    queries = jnp.dot(normed, query_full, preferred_element_type=jnp.float32)
    new_keys = jnp.dot(normed, key_full, preferred_element_type=jnp.float32).astype(jnp.bfloat16)
    new_values = jnp.dot(normed, value_full, preferred_element_type=jnp.float32).astype(
        jnp.bfloat16
    )
    prior_keys = kv_cache[0, 0]
    prior_values = kv_cache[0, 1]
    partner = lax.ppermute(
        (new_keys, new_values, prior_keys, prior_values),
        "gx",
        shift_pairs(lax.axis_size("gx"), 1, 2, 1),
    )
    all_keys = jnp.concatenate(
        [ordered(prior_keys, partner[2], is_first), ordered(new_keys, partner[0], is_first)], axis=0
    )
    all_values = jnp.concatenate(
        [ordered(prior_values, partner[3], is_first), ordered(new_values, partner[1], is_first)],
        axis=0,
    )
    prior_count = 2 * prior_keys.shape[0]
    query_pos = offset + jnp.arange(slot_count, dtype=jnp.int32)
    key_pos = jnp.arange(2 * slot_count, dtype=jnp.int32)
    allowed = jnp.concatenate(
        [jnp.ones((slot_count, prior_count), dtype=bool), key_pos[None, :] <= query_pos[:, None]],
        axis=1,
    )
    local_heads = queries.shape[1] // HD

    def split_heads(matrix):
        return matrix.reshape(matrix.shape[0], local_heads, HD).transpose(1, 0, 2)

    def one_head(operands):
        query_head, key_head, value_head = operands
        scores = jnp.einsum(
            "sd,kd->sk", query_head, key_head.astype(jnp.float32), precision=lax.Precision.HIGHEST
        ) * HD ** (-0.5)
        scores = jnp.where(allowed, scores, -jnp.inf)
        highest = jnp.max(scores, axis=1, keepdims=True)
        weights = jnp.exp(scores - highest)
        weight_sum = jnp.sum(weights, axis=1, keepdims=True)
        mixed_rows = jnp.dot(
            weights.astype(jnp.bfloat16), value_head, preferred_element_type=jnp.float32
        )
        return mixed_rows / weight_sum

    attended = lax.map(
        one_head, (split_heads(queries), split_heads(all_keys), split_heads(all_values))
    )
    attended = (
        attended.transpose(1, 0, 2).reshape(slot_count, local_heads * HD).astype(jnp.bfloat16)
    )
    attended_all = gather_gy(attended)
    attended_all = jnp.moveaxis(attended_all, 0, 1).reshape(slot_count, -1)
    residual = rows_full + jnp.dot(attended_all, out_full, preferred_element_type=jnp.float32)
    normed_two = normalized(residual).astype(jnp.bfloat16)
    expanded = jax.nn.gelu(
        jnp.dot(normed_two, expand_full, preferred_element_type=jnp.float32), approximate=True
    ).astype(jnp.bfloat16)
    contracted = lax.dot_general(
        expanded, contract_full_t, (((1,), (1,)), ((), ())), preferred_element_type=jnp.float32
    )
    groups = lax.axis_size("gy")
    own_width = D // groups
    blocks = contracted.reshape(slot_count, groups, own_width).transpose(1, 0, 2)
    summed = reduce_scatter_gy(blocks)
    column_start = lax.axis_index("gy") * own_width
    residual_own = lax.dynamic_slice_in_dim(residual, column_start, own_width, 1)
    is_valid = query_pos < lengths[prompt]
    output = jnp.where(is_valid[:, None], residual_own + summed, 0.0).astype(jnp.bfloat16)
    return (output, hand_over(kv_cache, prompt_group, page_table))


def solution(mesh):
    placed = (
        P("gx", None),
        P(),
        P("gx", "gy"),
        P("gx", "gy"),
        P("gx", "gy"),
        P("gy", "gx"),
        P("gx", "gy"),
        P("gy", "gx"),
        P(None, None, "gx", "gy"),
        P(),
        P(),
    )
    return jax.shard_map(
        on_device,
        mesh=mesh,
        in_specs=placed,
        out_specs=(P("gx", "gy"), P("gx", "gy", None, None, None)),
        check_vma=False,
    )
```

```python
import jax
import jax.numpy as jnp
from jax import lax
from jax.sharding import PartitionSpec as P

D = 1600
HD = 64
PRIOR = 768
PAGE = 128
POOL = 12


EPSILON = 1e-05

GX_CORE = (1, 2)
GX_Y = (2, 4)
GX_XLO = (8, 2)
GY_XHI = (1, 2)
GY_Z = (2, 4)


def shift_pairs(count, stride, size, step):
    pairs = []
    for i in range(count):
        c = (i // stride) % size
        j = i + (((c + step) % size) - c) * stride
        if j != i:
            pairs.append((i, j))
    return pairs


def sub_gather(block, axis, sub):
    stride, size = sub
    count = lax.axis_size(axis)
    c = (lax.axis_index(axis) // stride) % size
    if size == 2:
        other = lax.ppermute(block, axis, shift_pairs(count, stride, size, 1))
        got = jnp.stack([block, other])
    else:
        from_left = lax.ppermute(block, axis, shift_pairs(count, stride, size, 1))
        from_right = lax.ppermute(block, axis, shift_pairs(count, stride, size, -1))
        from_two = lax.ppermute(from_left, axis, shift_pairs(count, stride, size, 1))
        got = jnp.stack([block, from_left, from_two, from_right])
    order = (c - jnp.arange(size, dtype=jnp.int32)) % size
    return jnp.take(got, order, axis=0)


def gather_gx(block):
    g = sub_gather(block, "gx", GX_CORE)
    g = sub_gather(g, "gx", GX_XLO)
    g = sub_gather(g, "gx", GX_Y)
    g = jnp.swapaxes(g, 0, 1)
    return g.reshape((-1,) + block.shape)


def gather_gy(block):
    g = sub_gather(block, "gy", GY_XHI)
    g = sub_gather(g, "gy", GY_Z)
    return g.reshape((-1,) + block.shape)


def reduce_scatter_gy(blocks):
    count = lax.axis_size("gy")
    idx = lax.axis_index("gy")
    z = idx // 2
    h = idx % 2
    zsize = GY_Z[1]
    by_z = blocks.reshape((zsize, 2) + blocks.shape[1:])
    total = lax.dynamic_index_in_dim(by_z, z, 0, keepdims=False)
    for step in range(1, zsize):
        outgoing = lax.dynamic_index_in_dim(by_z, (z + step) % zsize, 0, keepdims=False)
        arrived = lax.ppermute(
            outgoing.astype(jnp.bfloat16), "gy", shift_pairs(count, GY_Z[0], zsize, step)
        )
        total = total + arrived.astype(jnp.float32)
    keep = lax.dynamic_index_in_dim(total, h, 0, keepdims=False)
    give = lax.dynamic_index_in_dim(total, 1 - h, 0, keepdims=False)
    arrived = lax.ppermute(give.astype(jnp.bfloat16), "gy", shift_pairs(count, 1, 2, 1))
    return keep + arrived.astype(jnp.float32)


def a2a_gather(block, axis):
    count = lax.axis_size(axis)
    copies = jnp.broadcast_to(block[None], (count,) + block.shape)
    return lax.all_to_all(copies, axis, 0, 0, tiled=True)


def finish_norm(row_block, row_sum, row_squares):
    average = row_sum / D
    variance = row_squares / D - average * average
    return (row_block - average) * lax.rsqrt(variance + EPSILON)


def normalized(row_block):
    return finish_norm(
        row_block,
        jnp.sum(row_block, axis=1, keepdims=True),
        jnp.sum(row_block * row_block, axis=1, keepdims=True),
    )


def ordered(own_part, other_part, is_first):
    lower_part = jnp.where(is_first, own_part, other_part)
    upper_part = jnp.where(is_first, other_part, own_part)
    return jnp.concatenate([lower_part, upper_part], axis=0)


def hand_over(kv_cache, prompt_group, page_table):
    moved_pages = lax.all_to_all(kv_cache, "gx", split_axis=0, concat_axis=2, tiled=True)
    columns = moved_pages.shape[3]
    pages_each = PRIOR // PAGE
    total_pages = moved_pages.shape[2] // PAGE
    groups = lax.axis_size("gy")
    page_ids = jnp.arange(total_pages, dtype=jnp.int32)
    destination = prompt_group[page_ids // pages_each] * POOL + page_table.reshape(-1)
    source = jnp.full((groups * POOL,), -1, jnp.int32).at[destination].set(page_ids)
    page_blocks = moved_pages.reshape(2, total_pages, PAGE, columns)
    picked = jnp.take(page_blocks, jnp.maximum(source, 0), axis=1)
    picked = jnp.where((source >= 0)[None, :, None, None], picked, jnp.zeros((), picked.dtype))
    picked = picked.reshape(2, groups, POOL * PAGE, columns)
    arrived = lax.all_to_all(picked, "gy", split_axis=1, concat_axis=1, tiled=True)
    arrived = jnp.concatenate([arrived[:, k] for k in range(groups)], axis=-1)
    return arrived.reshape(1, 1, 2, POOL * PAGE, columns * groups)


def on_device(
    hidden,
    lengths,
    query_weight,
    key_weight,
    value_weight,
    out_weight,
    expand_weight,
    contract_weight,
    kv_cache,
    prompt_group,
    page_table,
):
    slot_count = hidden.shape[0]
    device_row = lax.axis_index("gx")
    is_first = device_row % 2 == 0
    prompt = device_row // 2
    offset = device_row % 2 * slot_count
    local_cols = query_weight.shape[1]

    qkv_block = jnp.concatenate([query_weight, key_weight, value_weight], axis=1)
    qkv_full = a2a_gather(qkv_block, "gx").reshape(D, 3 * local_cols)
    query_full = qkv_full[:, :local_cols]
    key_full = qkv_full[:, local_cols : 2 * local_cols]
    value_full = qkv_full[:, 2 * local_cols :]

    ffn_block = jnp.concatenate([expand_weight, contract_weight.T], axis=1)
    qkv_full, ffn_block = lax.optimization_barrier((qkv_full, ffn_block))

    out_cols = jnp.moveaxis(gather_gx(out_weight), 0, 1).reshape(out_weight.shape[0], D)
    out_full = gather_gy(out_cols).reshape(-1, D)

    ffn_full = gather_gx(ffn_block).reshape(D, -1)
    ff_cols = expand_weight.shape[1]
    expand_full = ffn_full[:, :ff_cols]
    contract_full_t = ffn_full[:, ff_cols:]

    rows_full = hidden.astype(jnp.float32)
    normed = normalized(rows_full).astype(jnp.bfloat16)
    queries = jnp.dot(normed, query_full, preferred_element_type=jnp.float32)
    new_keys = jnp.dot(normed, key_full, preferred_element_type=jnp.float32).astype(jnp.bfloat16)
    new_values = jnp.dot(normed, value_full, preferred_element_type=jnp.float32).astype(
        jnp.bfloat16
    )
    prior_keys = kv_cache[0, 0]
    prior_values = kv_cache[0, 1]
    partner = lax.ppermute(
        (new_keys, new_values, prior_keys, prior_values),
        "gx",
        shift_pairs(lax.axis_size("gx"), 1, 2, 1),
    )
    partner, handover_cache = lax.optimization_barrier((partner, kv_cache))
    all_keys = jnp.concatenate(
        [ordered(prior_keys, partner[2], is_first), ordered(new_keys, partner[0], is_first)], axis=0
    )
    all_values = jnp.concatenate(
        [ordered(prior_values, partner[3], is_first), ordered(new_values, partner[1], is_first)],
        axis=0,
    )
    prior_count = 2 * prior_keys.shape[0]
    query_pos = offset + jnp.arange(slot_count, dtype=jnp.int32)
    key_pos = jnp.arange(2 * slot_count, dtype=jnp.int32)
    allowed = jnp.concatenate(
        [jnp.ones((slot_count, prior_count), dtype=bool), key_pos[None, :] <= query_pos[:, None]],
        axis=1,
    )
    local_heads = queries.shape[1] // HD

    def split_heads(matrix):
        return matrix.reshape(matrix.shape[0], local_heads, HD).transpose(1, 0, 2)

    def one_head(operands):
        query_head, key_head, value_head = operands
        scores = jnp.einsum(
            "sd,kd->sk", query_head, key_head.astype(jnp.float32), precision=lax.Precision.HIGHEST
        ) * HD ** (-0.5)
        scores = jnp.where(allowed, scores, -jnp.inf)
        highest = jnp.max(scores, axis=1, keepdims=True)
        weights = jnp.exp(scores - highest)
        weight_sum = jnp.sum(weights, axis=1, keepdims=True)
        mixed_rows = jnp.dot(
            weights.astype(jnp.bfloat16), value_head, preferred_element_type=jnp.float32
        )
        return mixed_rows / weight_sum

    attended = lax.map(
        one_head, (split_heads(queries), split_heads(all_keys), split_heads(all_values))
    )
    attended = (
        attended.transpose(1, 0, 2).reshape(slot_count, local_heads * HD).astype(jnp.bfloat16)
    )
    attended_all = gather_gy(attended)
    attended_all = jnp.moveaxis(attended_all, 0, 1).reshape(slot_count, -1)
    residual = rows_full + jnp.dot(attended_all, out_full, preferred_element_type=jnp.float32)
    normed_two = normalized(residual).astype(jnp.bfloat16)
    expanded = jax.nn.gelu(
        jnp.dot(normed_two, expand_full, preferred_element_type=jnp.float32), approximate=True
    ).astype(jnp.bfloat16)
    contracted = lax.dot_general(
        expanded, contract_full_t, (((1,), (1,)), ((), ())), preferred_element_type=jnp.float32
    )
    groups = lax.axis_size("gy")
    own_width = D // groups
    blocks = contracted.reshape(slot_count, groups, own_width).transpose(1, 0, 2)
    summed = reduce_scatter_gy(blocks)
    column_start = lax.axis_index("gy") * own_width
    residual_own = lax.dynamic_slice_in_dim(residual, column_start, own_width, 1)
    is_valid = query_pos < lengths[prompt]
    output = jnp.where(is_valid[:, None], residual_own + summed, 0.0).astype(jnp.bfloat16)
    return (output, hand_over(handover_cache, prompt_group, page_table))


def solution(mesh):
    placed = (
        P("gx", None),
        P(),
        P("gx", "gy"),
        P("gx", "gy"),
        P("gx", "gy"),
        P("gy", "gx"),
        P("gx", "gy"),
        P("gy", "gx"),
        P(None, None, "gx", "gy"),
        P(),
        P(),
    )
    return jax.shard_map(
        on_device,
        mesh=mesh,
        in_specs=placed,
        out_specs=(P("gx", "gy"), P("gx", "gy", None, None, None)),
        check_vma=False,
    )
```

```python
import jax
import jax.numpy as jnp
from jax import lax
from jax.sharding import PartitionSpec as P

D = 1600
HD = 64
PRIOR = 768
PAGE = 128
POOL = 12


EPSILON = 1e-05

GX_CORE = (1, 2)
GX_Y = (2, 4)
GX_XLO = (8, 2)
GY_XHI = (1, 2)
GY_Z = (2, 4)


def shift_pairs(count, stride, size, step):
    pairs = []
    for i in range(count):
        c = (i // stride) % size
        j = i + (((c + step) % size) - c) * stride
        if j != i:
            pairs.append((i, j))
    return pairs


def sub_gather(block, axis, sub):
    stride, size = sub
    count = lax.axis_size(axis)
    c = (lax.axis_index(axis) // stride) % size
    if size == 2:
        other = lax.ppermute(block, axis, shift_pairs(count, stride, size, 1))
        got = jnp.stack([block, other])
    else:
        from_left = lax.ppermute(block, axis, shift_pairs(count, stride, size, 1))
        from_right = lax.ppermute(block, axis, shift_pairs(count, stride, size, -1))
        from_two = lax.ppermute(from_left, axis, shift_pairs(count, stride, size, 1))
        got = jnp.stack([block, from_left, from_two, from_right])
    order = (c - jnp.arange(size, dtype=jnp.int32)) % size
    return jnp.take(got, order, axis=0)


def gather_gx(block):
    g = sub_gather(block, "gx", GX_CORE)
    g = sub_gather(g, "gx", GX_XLO)
    g = sub_gather(g, "gx", GX_Y)
    g = jnp.swapaxes(g, 0, 1)
    return g.reshape((-1,) + block.shape)


def gather_gy(block):
    g = sub_gather(block, "gy", GY_XHI)
    g = sub_gather(g, "gy", GY_Z)
    return g.reshape((-1,) + block.shape)


def reduce_scatter_gy(blocks):
    count = lax.axis_size("gy")
    idx = lax.axis_index("gy")
    z = idx // 2
    h = idx % 2
    zsize = GY_Z[1]
    by_z = blocks.reshape((zsize, 2) + blocks.shape[1:])
    total = lax.dynamic_index_in_dim(by_z, z, 0, keepdims=False)
    for step in range(1, zsize):
        outgoing = lax.dynamic_index_in_dim(by_z, (z + step) % zsize, 0, keepdims=False)
        arrived = lax.ppermute(
            outgoing.astype(jnp.bfloat16), "gy", shift_pairs(count, GY_Z[0], zsize, step)
        )
        total = total + arrived.astype(jnp.float32)
    keep = lax.dynamic_index_in_dim(total, h, 0, keepdims=False)
    give = lax.dynamic_index_in_dim(total, 1 - h, 0, keepdims=False)
    arrived = lax.ppermute(give.astype(jnp.bfloat16), "gy", shift_pairs(count, 1, 2, 1))
    return keep + arrived.astype(jnp.float32)


def a2a_gather(block, axis):
    count = lax.axis_size(axis)
    copies = jnp.broadcast_to(block[None], (count,) + block.shape)
    return lax.all_to_all(copies, axis, 0, 0, tiled=True)


def finish_norm(row_block, row_sum, row_squares):
    average = row_sum / D
    variance = row_squares / D - average * average
    return (row_block - average) * lax.rsqrt(variance + EPSILON)


def normalized(row_block):
    return finish_norm(
        row_block,
        jnp.sum(row_block, axis=1, keepdims=True),
        jnp.sum(row_block * row_block, axis=1, keepdims=True),
    )


def ordered(own_part, other_part, is_first):
    lower_part = jnp.where(is_first, own_part, other_part)
    upper_part = jnp.where(is_first, other_part, own_part)
    return jnp.concatenate([lower_part, upper_part], axis=0)


def hand_over(kv_cache, prompt_group, page_table):
    moved_pages = lax.all_to_all(kv_cache, "gx", split_axis=0, concat_axis=2, tiled=True)
    columns = moved_pages.shape[3]
    pages_each = PRIOR // PAGE
    total_pages = moved_pages.shape[2] // PAGE
    groups = lax.axis_size("gy")
    page_ids = jnp.arange(total_pages, dtype=jnp.int32)
    destination = prompt_group[page_ids // pages_each] * POOL + page_table.reshape(-1)
    source = jnp.full((groups * POOL,), -1, jnp.int32).at[destination].set(page_ids)
    page_blocks = moved_pages.reshape(2, total_pages, PAGE, columns)
    picked = jnp.take(page_blocks, jnp.maximum(source, 0), axis=1)
    picked = jnp.where((source >= 0)[None, :, None, None], picked, jnp.zeros((), picked.dtype))
    picked = picked.reshape(2, groups, POOL * PAGE, columns)
    arrived = lax.all_to_all(picked, "gy", split_axis=1, concat_axis=1, tiled=True)
    arrived = jnp.concatenate([arrived[:, k] for k in range(groups)], axis=-1)
    return arrived.reshape(1, 1, 2, POOL * PAGE, columns * groups)


def on_device(
    hidden,
    lengths,
    query_weight,
    key_weight,
    value_weight,
    out_weight,
    expand_weight,
    contract_weight,
    kv_cache,
    prompt_group,
    page_table,
):
    slot_count = hidden.shape[0]
    device_row = lax.axis_index("gx")
    is_first = device_row % 2 == 0
    prompt = device_row // 2
    offset = device_row % 2 * slot_count
    local_cols = query_weight.shape[1]

    qkv_block = jnp.concatenate([query_weight, key_weight, value_weight], axis=1)
    qkv_full = a2a_gather(qkv_block, "gx").reshape(D, 3 * local_cols)
    query_full = qkv_full[:, :local_cols]
    key_full = qkv_full[:, local_cols : 2 * local_cols]
    value_full = qkv_full[:, 2 * local_cols :]

    ffn_block = jnp.concatenate([expand_weight, contract_weight.T], axis=1)
    qkv_full, ffn_block, kv_cache = lax.optimization_barrier((qkv_full, ffn_block, kv_cache))

    out_cols = jnp.moveaxis(gather_gx(out_weight), 0, 1).reshape(out_weight.shape[0], D)
    out_full = gather_gy(out_cols).reshape(-1, D)

    ffn_full = gather_gx(ffn_block).reshape(D, -1)
    ff_cols = expand_weight.shape[1]
    expand_full = ffn_full[:, :ff_cols]
    contract_full_t = ffn_full[:, ff_cols:]

    rows_full = hidden.astype(jnp.float32)
    normed = normalized(rows_full).astype(jnp.bfloat16)
    queries = jnp.dot(normed, query_full, preferred_element_type=jnp.float32)
    new_keys = jnp.dot(normed, key_full, preferred_element_type=jnp.float32).astype(jnp.bfloat16)
    new_values = jnp.dot(normed, value_full, preferred_element_type=jnp.float32).astype(
        jnp.bfloat16
    )
    prior_keys = kv_cache[0, 0]
    prior_values = kv_cache[0, 1]
    partner = lax.ppermute(
        (new_keys, new_values, prior_keys, prior_values),
        "gx",
        shift_pairs(lax.axis_size("gx"), 1, 2, 1),
    )
    all_keys = jnp.concatenate(
        [ordered(prior_keys, partner[2], is_first), ordered(new_keys, partner[0], is_first)], axis=0
    )
    all_values = jnp.concatenate(
        [ordered(prior_values, partner[3], is_first), ordered(new_values, partner[1], is_first)],
        axis=0,
    )
    prior_count = 2 * prior_keys.shape[0]
    query_pos = offset + jnp.arange(slot_count, dtype=jnp.int32)
    key_pos = jnp.arange(2 * slot_count, dtype=jnp.int32)
    allowed = jnp.concatenate(
        [jnp.ones((slot_count, prior_count), dtype=bool), key_pos[None, :] <= query_pos[:, None]],
        axis=1,
    )
    local_heads = queries.shape[1] // HD

    def split_heads(matrix):
        return matrix.reshape(matrix.shape[0], local_heads, HD).transpose(1, 0, 2)

    def one_head(operands):
        query_head, key_head, value_head = operands
        scores = jnp.einsum(
            "sd,kd->sk", query_head, key_head.astype(jnp.float32), precision=lax.Precision.HIGHEST
        ) * HD ** (-0.5)
        scores = jnp.where(allowed, scores, -jnp.inf)
        highest = jnp.max(scores, axis=1, keepdims=True)
        weights = jnp.exp(scores - highest)
        weight_sum = jnp.sum(weights, axis=1, keepdims=True)
        mixed_rows = jnp.dot(
            weights.astype(jnp.bfloat16), value_head, preferred_element_type=jnp.float32
        )
        return mixed_rows / weight_sum

    attended = lax.map(
        one_head, (split_heads(queries), split_heads(all_keys), split_heads(all_values))
    )
    attended = (
        attended.transpose(1, 0, 2).reshape(slot_count, local_heads * HD).astype(jnp.bfloat16)
    )
    attended_all = gather_gy(attended)
    attended_all = jnp.moveaxis(attended_all, 0, 1).reshape(slot_count, -1)
    residual = rows_full + jnp.dot(attended_all, out_full, preferred_element_type=jnp.float32)
    normed_two = normalized(residual).astype(jnp.bfloat16)
    expanded = jax.nn.gelu(
        jnp.dot(normed_two, expand_full, preferred_element_type=jnp.float32), approximate=True
    ).astype(jnp.bfloat16)
    contracted = lax.dot_general(
        expanded, contract_full_t, (((1,), (1,)), ((), ())), preferred_element_type=jnp.float32
    )
    groups = lax.axis_size("gy")
    own_width = D // groups
    blocks = contracted.reshape(slot_count, groups, own_width).transpose(1, 0, 2)
    summed = reduce_scatter_gy(blocks)
    column_start = lax.axis_index("gy") * own_width
    residual_own = lax.dynamic_slice_in_dim(residual, column_start, own_width, 1)
    is_valid = query_pos < lengths[prompt]
    output = jnp.where(is_valid[:, None], residual_own + summed, 0.0).astype(jnp.bfloat16)
    return (output, hand_over(kv_cache, prompt_group, page_table))


def solution(mesh):
    placed = (
        P("gx", None),
        P(),
        P("gx", "gy"),
        P("gx", "gy"),
        P("gx", "gy"),
        P("gy", "gx"),
        P("gx", "gy"),
        P("gy", "gx"),
        P(None, None, "gx", "gy"),
        P(),
        P(),
    )
    return jax.shard_map(
        on_device,
        mesh=mesh,
        in_specs=placed,
        out_specs=(P("gx", "gy"), P("gx", "gy", None, None, None)),
        check_vma=False,
    )
```
